512 devices in a mesh: az: 128 (over x, z_lo, y), rad: 4 (over z_hi, core).
Axes of the slice: x: 4, y: 4, z: 16 (z_hi: 2, z_lo: 8; z = z_hi * 8 + z_lo), core: 2. Of those that a mesh axis runs over, the one named last changes fastest.
Arguments:
- block_mass: float32 [128, 4, 512, 128], P('az', 'rad'), may hold values from 0.5 to 4
- block_flux: float32 [128, 4, 512, 9, 128], P('az', 'rad'), may hold values from -6 to 6
- block_dest: int32 [128, 4, 512], P('az', 'rad'), may hold values from 0 to 32767, as said below
- block_count: int32 [128, 4], P('az', 'rad'), may hold values from 128 to 512, as said below
Outputs:
- smoothed: float32 [10, 1024, 32, 512], P(None, 'az', None, 'rad')
- force: float32 [3, 1024, 32, 512], P(None, 'az', None, 'rad')
- strain: float32 [6, 1024, 32, 512], P(None, 'az', None, 'rad')
The draws below stay inside these ranges and needn't reach their ends.
Inputs may be any that keep to these rules, and one draw needn't show every extreme that they name: `block_dest`: the azimuthal row of a block of device (a, b) lies from 2 rows before to 2 rows after the rows a * 8 to a * 8 + 7, cyclically over 1024 rows. `block_count`: some device is full in every draw.
All inputs are finite; a program needn't handle non-finite values.
Results may differ from the reference program's by a relative error of at most 0.000076.
Values sent between devices are 32-bit elements; how exact they have to be, the bound alone decides.
No kernel may reach another device: no remote copies, remote signals or barrier semaphores. Data moves between devices by JAX's collectives and lax.ppermute only.
A program may use at most 64 MiB of HBM per device.

```python
import math
import jax
import jax.numpy as jnp

CA = 8
H = 32
CR = 128
SLOTS = 512
NA = 1024
NR = 512
N_AZ = 128
N_RAD = 4


def draw_block_dest(key, part):
    first, second = jax.random.split(key)
    offset_rows = jax.random.randint(first, (N_AZ, N_RAD, SLOTS), -2, CA + 2)
    height_cell = jax.random.randint(second, (N_AZ, N_RAD, SLOTS), 0, H)
    offset_rows = offset_rows.at[0, 0, 0].set(-1).at[0, 0, 1].set(0)
    height_cell = height_cell.at[0, 0, 0].set(H - 1).at[0, 0, 1].set(0)
    sector_start = jnp.arange(N_AZ, dtype=jnp.int32)[:, None, None] * CA
    row_index = jnp.mod(sector_start + offset_rows, CA * N_AZ)
    return (row_index * H + height_cell).astype(jnp.int32)


def draw_block_count(key, part):
    first, second = jax.random.split(key)
    total = N_AZ * N_RAD
    counts = jax.random.randint(first, (total,), SLOTS // 4, SLOTS + 1)
    chosen = jax.random.randint(second, (), 0, total)
    device_ids = jnp.arange(total, dtype=jnp.int32)
    filled = jnp.where(device_ids == chosen, SLOTS, counts)
    filled = jnp.where(device_ids == jnp.mod(chosen + 1, total), SLOTS // 4, filled)
    return filled.reshape(N_AZ, N_RAD).astype(jnp.int32)


def steps_of(rng, dims, shards, least, high):
    factor_of = 1.0
    for dim, blocks in shards:
        draws = jax.random.uniform(jax.random.fold_in(jax.random.fold_in(rng, 6), dim), (blocks,), jnp.float32, least / len(shards), high / len(shards))
        factor_of = factor_of * jnp.repeat(jnp.exp(draws), dims[dim] // blocks).reshape((-1,) + (1,) * (len(dims) - 1 - dim))
    return factor_of


def bell_draw(rng, dims, width, reach, cuts=(), held_as=jnp.bfloat16):
    array = width * jax.random.normal(rng, dims, jnp.float32)
    if cuts:
        array = array * steps_of(rng, dims, cuts, -0.22, 0.18)
    return jnp.clip(array, -reach, reach).astype(held_as)


def setup_inputs(seed: int = 0) -> dict:
    seeds = jax.random.split(jax.random.key(seed), 5)
    block_mass = jnp.clip(jnp.exp(math.log(4.0) - 2.0794415 * jax.random.uniform(seeds[0], (N_AZ, N_RAD, SLOTS, CR), jnp.float32) ** steps_of(seeds[0], (N_AZ, N_RAD, SLOTS, CR), ((0, 128), (1, 4)), -0.2, 0.2)), 0.5, 4.0)
    block_flux = bell_draw(seeds[1], (N_AZ, N_RAD, SLOTS, 9, CR), 1.0, 6.0, ((0, 128), (1, 4)), jnp.float32)
    block_dest = draw_block_dest(jax.random.fold_in(seeds[4], 71), 0)
    block_count = draw_block_count(jax.random.fold_in(seeds[4], 71), 0)
    return dict(block_mass=block_mass, block_flux=block_flux, block_dest=block_dest, block_count=block_count)


density_base = 0.5


def smooth_grid(fields):
    fields = 0.25 * jnp.roll(fields, 1, 1) + 0.5 * fields + 0.25 * jnp.roll(fields, -1, 1)
    padded = jnp.pad(fields, ((0, 0), (0, 0), (0, 0), (1, 1)))
    fields = 0.25 * padded[..., :-2] + 0.5 * padded[..., 1:-1] + 0.25 * padded[..., 2:]
    padded = jnp.pad(fields, ((0, 0), (0, 0), (1, 1), (0, 0)))
    return 0.25 * padded[:, :, :-2] + 0.5 * padded[:, :, 1:-1] + 0.25 * padded[:, :, 2:]


def assemble(grad_az, grad_height, grad_rad, center, recip):
    force = jnp.stack([grad_az[3] + grad_height[6] + grad_rad[7] + 2.0 * center[7] * recip,
                       grad_az[6] + grad_height[4] + grad_rad[8],
                       grad_az[7] + grad_height[8] + grad_rad[5] + (center[5] - center[3]) * recip])
    strain = jnp.stack([grad_az[0] + center[2] * recip, grad_height[1], grad_rad[2],
                        0.5 * (grad_height[0] + grad_az[1]),
                        0.5 * (grad_rad[0] + grad_az[2] - center[0] * recip),
                        0.5 * (grad_rad[1] + grad_height[2])])
    return force, strain


def reference(block_mass, block_flux, block_dest, block_count):
    values = jnp.concatenate([block_mass[:, :, :, None, :], block_flux], axis=3)
    live = (jnp.arange(SLOTS, dtype=jnp.int32)[None, None, :] < block_count[:, :, None]).astype(jnp.float32)
    band_index = jnp.arange(N_RAD, dtype=jnp.int32)[None, :, None]
    target = (block_dest * N_RAD + band_index).astype(jnp.int32)
    summed = jax.ops.segment_sum((values * live[..., None, None]).reshape(-1, 10, CR),
                                 target.reshape(-1), num_segments=NA * H * N_RAD)
    fields = summed.reshape(NA, H, N_RAD, 10, CR).transpose(3, 0, 1, 2, 4).reshape(10, NA, H, NR)
    smoothed = smooth_grid(fields)
    velocity = smoothed[1:4] / (smoothed[0:1] + density_base)
    combined = jnp.concatenate([velocity, smoothed[4:]], axis=0)
    radius = NR + jnp.arange(NR, dtype=jnp.float32) + 0.5
    dtheta = 2.0 * math.pi / NA
    scale_az = 0.5 / (radius * dtheta)
    recip = 1.0 / radius
    grad_az = (jnp.roll(combined, -1, 1) - jnp.roll(combined, 1, 1)) * scale_az
    padded = jnp.pad(combined, ((0, 0), (0, 0), (0, 0), (1, 1)))
    grad_rad = (padded[..., 2:] - padded[..., :-2]) * 0.5
    padded = jnp.pad(combined, ((0, 0), (0, 0), (1, 1), (0, 0)))
    grad_height = (padded[:, :, 2:] - padded[:, :, :-2]) * 0.5
    force, strain = assemble(grad_az, grad_height, grad_rad, combined, recip)
    return smoothed, force, strain
```

```python
import math

import jax
import jax.numpy as jnp
from jax import lax
from jax.sharding import PartitionSpec as P

CA = 8
H = 32
HALO = 2


density_base = 0.5


def shifted(value, da, db):
    n_az = lax.axis_size("az")
    n_rad = lax.axis_size("rad")
    pairs = []
    for a in range(n_az):
        for b in range(n_rad):
            tb = b + db
            if 0 <= tb < n_rad:
                pairs.append((a * n_rad + b, ((a + da) % n_az) * n_rad + tb))
    return lax.ppermute(value, ("az", "rad"), pairs)


def deposit(onehot, values):
    return jnp.einsum("ls,scn->cln", onehot, values, precision=lax.Precision.HIGHEST)


def local_rows(values, dest, live, start, total_rows, width):
    local_row = jnp.mod(dest // H - start + HALO, total_rows)
    line = local_row * H + dest % H
    onehot = (
        (jnp.arange((CA + 2 * HALO) * H, dtype=jnp.int32)[:, None] == line[None, :]) & live[None, :]
    ).astype(jnp.float32)
    return deposit(onehot, values).reshape(10, CA + 2 * HALO, H, width)


def add_rows(base, head, tail):
    k = head.shape[1]
    rows = base.shape[1]
    return jnp.concatenate(
        [base[:, :k] + head, base[:, k : rows - k], base[:, rows - k :] + tail], axis=1
    )


def window(raw):
    k = 2 * HALO
    top = raw[:, :k]
    bottom = raw[:, -k:]
    center = add_rows(raw, shifted(bottom, 1, 0), shifted(top, -1, 0))
    lo = slice(0, HALO)
    hi = slice(raw.shape[3] - HALO, raw.shape[3])
    right = add_rows(
        shifted(raw[..., lo], 0, -1),
        shifted(bottom[..., lo], 1, -1),
        shifted(top[..., lo], -1, -1),
    )
    left = add_rows(
        shifted(raw[..., hi], 0, 1),
        shifted(bottom[..., hi], 1, 1),
        shifted(top[..., hi], -1, 1),
    )
    return jnp.concatenate([left, center, right], axis=3)


def smooth_block(extended):
    fields = 0.25 * extended[:, :-2] + 0.5 * extended[:, 1:-1] + 0.25 * extended[:, 2:]
    fields = 0.25 * fields[..., :-2] + 0.5 * fields[..., 1:-1] + 0.25 * fields[..., 2:]
    padded = jnp.pad(fields, ((0, 0), (0, 0), (1, 1), (0, 0)))
    return 0.25 * padded[:, :, :-2] + 0.5 * padded[:, :, 1:-1] + 0.25 * padded[:, :, 2:]


def radial_mask(extended, depth, band_index, width, n_rad):
    columns = band_index * width - depth + jnp.arange(width + 2 * depth, dtype=jnp.int32)
    inside = (columns >= 0) & (columns < width * n_rad)
    return extended * inside.astype(jnp.float32)


def gradients(extended, scale_az):
    center = extended[:, 1:-1, :, 1:-1]
    grad_az = (extended[:, 2:, :, 1:-1] - extended[:, :-2, :, 1:-1]) * scale_az
    grad_rad = (extended[:, 1:-1, :, 2:] - extended[:, 1:-1, :, :-2]) * 0.5
    padded = jnp.pad(center, ((0, 0), (0, 0), (1, 1), (0, 0)))
    grad_height = (padded[:, :, 2:] - padded[:, :, :-2]) * 0.5
    return (grad_az, grad_height, grad_rad, center)


def assemble(grad_az, grad_height, grad_rad, center, recip):
    force = jnp.stack(
        [
            grad_az[3] + grad_height[6] + grad_rad[7] + 2.0 * center[7] * recip,
            grad_az[6] + grad_height[4] + grad_rad[8],
            grad_az[7] + grad_height[8] + grad_rad[5] + (center[5] - center[3]) * recip,
        ]
    )
    strain = jnp.stack(
        [
            grad_az[0] + center[2] * recip,
            grad_height[1],
            grad_rad[2],
            0.5 * (grad_height[0] + grad_az[1]),
            0.5 * (grad_rad[0] + grad_az[2] - center[0] * recip),
            0.5 * (grad_rad[1] + grad_height[2]),
        ]
    )
    return (force, strain)


def local(block_mass, block_flux, block_dest, block_count):
    sector = lax.axis_index("az")
    band_index = lax.axis_index("rad")
    n_az = lax.axis_size("az")
    n_rad = lax.axis_size("rad")
    slots = block_mass.shape[2]
    width = block_mass.shape[3]
    total_rows = CA * n_az
    start = sector * CA
    values = jnp.concatenate([block_mass[0, 0][:, None, :], block_flux[0, 0]], axis=1)
    dest = block_dest[0, 0]
    slot_index = jnp.arange(slots, dtype=jnp.int32)
    live = slot_index < block_count[0, 0]
    raw = local_rows(values, dest, live, start, total_rows, width)
    extended = window(raw)
    glob_cells = (band_index * width + jnp.arange(width, dtype=jnp.int32)).astype(jnp.float32)
    radius = width * n_rad + glob_cells + 0.5
    dtheta = 2.0 * math.pi / total_rows
    scale_az = 0.5 / (radius * dtheta)
    recip = 1.0 / radius
    smoothed_ext = smooth_block(extended)
    smoothed = smoothed_ext[:, 1:-1, :, 1:-1]
    velocity = smoothed_ext[1:4] / (smoothed_ext[0:1] + density_base)
    combined = jnp.concatenate([velocity, smoothed_ext[4:]], axis=0)
    combined = radial_mask(combined, 1, band_index, width, n_rad)
    grad_az, grad_height, grad_rad, center = gradients(combined, scale_az)
    force, strain = assemble(grad_az, grad_height, grad_rad, center, recip)
    return (smoothed, force, strain)


def solution(mesh):
    return jax.shard_map(
        local,
        mesh=mesh,
        in_specs=(
            P("az", "rad", None, None),
            P("az", "rad", None, None, None),
            P("az", "rad", None),
            P("az", "rad"),
        ),
        out_specs=(
            P(None, "az", None, "rad"),
            P(None, "az", None, "rad"),
            P(None, "az", None, "rad"),
        ),
        check_vma=False,
    )
```

```python
import math

import jax
import jax.numpy as jnp
from jax import lax
from jax.sharding import PartitionSpec as P

CA = 8
H = 32
HALO = 2


density_base = 0.5


def shifted(value, da, db):
    n_az = lax.axis_size("az")
    n_rad = lax.axis_size("rad")
    pairs = []
    for a in range(n_az):
        for b in range(n_rad):
            tb = b + db
            if 0 <= tb < n_rad:
                pairs.append((a * n_rad + b, ((a + da) % n_az) * n_rad + tb))
    return lax.ppermute(value, ("az", "rad"), pairs)


def deposit(onehot, values):
    return jnp.einsum("ls,scn->cln", onehot, values, precision=lax.Precision.HIGHEST)


def local_rows(values, dest, live, start, total_rows, width):
    local_row = jnp.mod(dest // H - start + HALO, total_rows)
    line = local_row * H + dest % H
    onehot = (
        (jnp.arange((CA + 2 * HALO) * H, dtype=jnp.int32)[:, None] == line[None, :]) & live[None, :]
    ).astype(jnp.float32)
    return deposit(onehot, values).reshape(10, CA + 2 * HALO, H, width)


def add_rows(base, head, tail):
    k = head.shape[1]
    rows = base.shape[1]
    return jnp.concatenate(
        [base[:, :k] + head, base[:, k : rows - k], base[:, rows - k :] + tail], axis=1
    )


def window(raw):
    cells = raw.shape[3]
    right = shifted(raw[..., :HALO], 0, -1)
    left = shifted(raw[..., cells - HALO :], 0, 1)
    wide = jnp.concatenate([left, raw, right], axis=3)
    k = 2 * HALO
    return add_rows(wide, shifted(wide[:, -k:], 1, 0), shifted(wide[:, :k], -1, 0))


def smooth_block(extended):
    fields = 0.25 * extended[:, :-2] + 0.5 * extended[:, 1:-1] + 0.25 * extended[:, 2:]
    fields = 0.25 * fields[..., :-2] + 0.5 * fields[..., 1:-1] + 0.25 * fields[..., 2:]
    padded = jnp.pad(fields, ((0, 0), (0, 0), (1, 1), (0, 0)))
    return 0.25 * padded[:, :, :-2] + 0.5 * padded[:, :, 1:-1] + 0.25 * padded[:, :, 2:]


def radial_mask(extended, depth, band_index, width, n_rad):
    columns = band_index * width - depth + jnp.arange(width + 2 * depth, dtype=jnp.int32)
    inside = (columns >= 0) & (columns < width * n_rad)
    return extended * inside.astype(jnp.float32)


def gradients(extended, scale_az):
    center = extended[:, 1:-1, :, 1:-1]
    grad_az = (extended[:, 2:, :, 1:-1] - extended[:, :-2, :, 1:-1]) * scale_az
    grad_rad = (extended[:, 1:-1, :, 2:] - extended[:, 1:-1, :, :-2]) * 0.5
    padded = jnp.pad(center, ((0, 0), (0, 0), (1, 1), (0, 0)))
    grad_height = (padded[:, :, 2:] - padded[:, :, :-2]) * 0.5
    return (grad_az, grad_height, grad_rad, center)


def assemble(grad_az, grad_height, grad_rad, center, recip):
    force = jnp.stack(
        [
            grad_az[3] + grad_height[6] + grad_rad[7] + 2.0 * center[7] * recip,
            grad_az[6] + grad_height[4] + grad_rad[8],
            grad_az[7] + grad_height[8] + grad_rad[5] + (center[5] - center[3]) * recip,
        ]
    )
    strain = jnp.stack(
        [
            grad_az[0] + center[2] * recip,
            grad_height[1],
            grad_rad[2],
            0.5 * (grad_height[0] + grad_az[1]),
            0.5 * (grad_rad[0] + grad_az[2] - center[0] * recip),
            0.5 * (grad_rad[1] + grad_height[2]),
        ]
    )
    return (force, strain)


def local(block_mass, block_flux, block_dest, block_count):
    sector = lax.axis_index("az")
    band_index = lax.axis_index("rad")
    n_az = lax.axis_size("az")
    n_rad = lax.axis_size("rad")
    slots = block_mass.shape[2]
    width = block_mass.shape[3]
    total_rows = CA * n_az
    start = sector * CA
    values = jnp.concatenate([block_mass[0, 0][:, None, :], block_flux[0, 0]], axis=1)
    dest = block_dest[0, 0]
    slot_index = jnp.arange(slots, dtype=jnp.int32)
    live = slot_index < block_count[0, 0]
    raw = local_rows(values, dest, live, start, total_rows, width)
    extended = window(raw)
    glob_cells = (band_index * width + jnp.arange(width, dtype=jnp.int32)).astype(jnp.float32)
    radius = width * n_rad + glob_cells + 0.5
    dtheta = 2.0 * math.pi / total_rows
    scale_az = 0.5 / (radius * dtheta)
    recip = 1.0 / radius
    smoothed_ext = smooth_block(extended)
    smoothed = smoothed_ext[:, 1:-1, :, 1:-1]
    velocity = smoothed_ext[1:4] / (smoothed_ext[0:1] + density_base)
    combined = jnp.concatenate([velocity, smoothed_ext[4:]], axis=0)
    combined = radial_mask(combined, 1, band_index, width, n_rad)
    grad_az, grad_height, grad_rad, center = gradients(combined, scale_az)
    force, strain = assemble(grad_az, grad_height, grad_rad, center, recip)
    return (smoothed, force, strain)


def solution(mesh):
    return jax.shard_map(
        local,
        mesh=mesh,
        in_specs=(
            P("az", "rad", None, None),
            P("az", "rad", None, None, None),
            P("az", "rad", None),
            P("az", "rad"),
        ),
        out_specs=(
            P(None, "az", None, "rad"),
            P(None, "az", None, "rad"),
            P(None, "az", None, "rad"),
        ),
        check_vma=False,
    )
```

```python
import math

import jax
import jax.numpy as jnp
from jax import lax
from jax.sharding import PartitionSpec as P

CA = 8
H = 32
HALO = 2


density_base = 0.5


def shifted(value, da, db):
    n_az = lax.axis_size("az")
    n_rad = lax.axis_size("rad")
    pairs = []
    for a in range(n_az):
        for b in range(n_rad):
            tb = b + db
            if 0 <= tb < n_rad:
                pairs.append((a * n_rad + b, ((a + da) % n_az) * n_rad + tb))
    shape = value.shape
    dense = value.reshape(value.size // 128, 128)
    return lax.ppermute(dense, ("az", "rad"), pairs).reshape(shape)


def deposit(onehot, values):
    return jnp.einsum("ls,scn->cln", onehot, values, precision=lax.Precision.HIGHEST)


def local_rows(values, dest, live, start, total_rows, width):
    local_row = jnp.mod(dest // H - start + HALO, total_rows)
    line = local_row * H + dest % H
    onehot = (
        (jnp.arange((CA + 2 * HALO) * H, dtype=jnp.int32)[:, None] == line[None, :]) & live[None, :]
    ).astype(jnp.float32)
    return deposit(onehot, values).reshape(10, CA + 2 * HALO, H, width)


def add_rows(base, head, tail):
    k = head.shape[1]
    rows = base.shape[1]
    return jnp.concatenate(
        [base[:, :k] + head, base[:, k : rows - k], base[:, rows - k :] + tail], axis=1
    )


def window(raw):
    cells = raw.shape[3]
    right = shifted(raw[..., :HALO], 0, -1)
    left = shifted(raw[..., cells - HALO :], 0, 1)
    wide = jnp.concatenate([left, raw, right], axis=3)
    k = 2 * HALO
    return add_rows(wide, shifted(wide[:, -k:], 1, 0), shifted(wide[:, :k], -1, 0))


def smooth_block(extended):
    fields = 0.25 * extended[:, :-2] + 0.5 * extended[:, 1:-1] + 0.25 * extended[:, 2:]
    fields = 0.25 * fields[..., :-2] + 0.5 * fields[..., 1:-1] + 0.25 * fields[..., 2:]
    padded = jnp.pad(fields, ((0, 0), (0, 0), (1, 1), (0, 0)))
    return 0.25 * padded[:, :, :-2] + 0.5 * padded[:, :, 1:-1] + 0.25 * padded[:, :, 2:]


def radial_mask(extended, depth, band_index, width, n_rad):
    columns = band_index * width - depth + jnp.arange(width + 2 * depth, dtype=jnp.int32)
    inside = (columns >= 0) & (columns < width * n_rad)
    return extended * inside.astype(jnp.float32)


def gradients(extended, scale_az):
    center = extended[:, 1:-1, :, 1:-1]
    grad_az = (extended[:, 2:, :, 1:-1] - extended[:, :-2, :, 1:-1]) * scale_az
    grad_rad = (extended[:, 1:-1, :, 2:] - extended[:, 1:-1, :, :-2]) * 0.5
    padded = jnp.pad(center, ((0, 0), (0, 0), (1, 1), (0, 0)))
    grad_height = (padded[:, :, 2:] - padded[:, :, :-2]) * 0.5
    return (grad_az, grad_height, grad_rad, center)


def assemble(grad_az, grad_height, grad_rad, center, recip):
    force = jnp.stack(
        [
            grad_az[3] + grad_height[6] + grad_rad[7] + 2.0 * center[7] * recip,
            grad_az[6] + grad_height[4] + grad_rad[8],
            grad_az[7] + grad_height[8] + grad_rad[5] + (center[5] - center[3]) * recip,
        ]
    )
    strain = jnp.stack(
        [
            grad_az[0] + center[2] * recip,
            grad_height[1],
            grad_rad[2],
            0.5 * (grad_height[0] + grad_az[1]),
            0.5 * (grad_rad[0] + grad_az[2] - center[0] * recip),
            0.5 * (grad_rad[1] + grad_height[2]),
        ]
    )
    return (force, strain)


def local(block_mass, block_flux, block_dest, block_count):
    sector = lax.axis_index("az")
    band_index = lax.axis_index("rad")
    n_az = lax.axis_size("az")
    n_rad = lax.axis_size("rad")
    slots = block_mass.shape[2]
    width = block_mass.shape[3]
    total_rows = CA * n_az
    start = sector * CA
    values = jnp.concatenate([block_mass[0, 0][:, None, :], block_flux[0, 0]], axis=1)
    dest = block_dest[0, 0]
    slot_index = jnp.arange(slots, dtype=jnp.int32)
    live = slot_index < block_count[0, 0]
    raw = local_rows(values, dest, live, start, total_rows, width)
    extended = window(raw)
    glob_cells = (band_index * width + jnp.arange(width, dtype=jnp.int32)).astype(jnp.float32)
    radius = width * n_rad + glob_cells + 0.5
    dtheta = 2.0 * math.pi / total_rows
    scale_az = 0.5 / (radius * dtheta)
    recip = 1.0 / radius
    smoothed_ext = smooth_block(extended)
    smoothed = smoothed_ext[:, 1:-1, :, 1:-1]
    velocity = smoothed_ext[1:4] / (smoothed_ext[0:1] + density_base)
    combined = jnp.concatenate([velocity, smoothed_ext[4:]], axis=0)
    combined = radial_mask(combined, 1, band_index, width, n_rad)
    grad_az, grad_height, grad_rad, center = gradients(combined, scale_az)
    force, strain = assemble(grad_az, grad_height, grad_rad, center, recip)
    return (smoothed, force, strain)


def solution(mesh):
    return jax.shard_map(
        local,
        mesh=mesh,
        in_specs=(
            P("az", "rad", None, None),
            P("az", "rad", None, None, None),
            P("az", "rad", None),
            P("az", "rad"),
        ),
        out_specs=(
            P(None, "az", None, "rad"),
            P(None, "az", None, "rad"),
            P(None, "az", None, "rad"),
        ),
        check_vma=False,
    )
```

```python
import math

import jax
import jax.numpy as jnp
from jax import lax
from jax.sharding import PartitionSpec as P

CA = 8
H = 32
HALO = 2


density_base = 0.5


def shifted(value, da, db):
    n_az = lax.axis_size("az")
    n_rad = lax.axis_size("rad")
    pairs = []
    for a in range(n_az):
        for b in range(n_rad):
            tb = b + db
            if 0 <= tb < n_rad:
                pairs.append((a * n_rad + b, ((a + da) % n_az) * n_rad + tb))
    shape = value.shape
    if shape[-1] % 128 == 0:
        return lax.ppermute(value, ("az", "rad"), pairs)
    dense = value.reshape(value.size // 128, 128)
    return lax.ppermute(dense, ("az", "rad"), pairs).reshape(shape)


def deposit(onehot, values):
    return jnp.einsum("ls,scn->cln", onehot, values, precision=lax.Precision.HIGHEST)


def local_rows(values, dest, live, start, total_rows, width):
    local_row = jnp.mod(dest // H - start + HALO, total_rows)
    line = local_row * H + dest % H
    onehot = (
        (jnp.arange((CA + 2 * HALO) * H, dtype=jnp.int32)[:, None] == line[None, :]) & live[None, :]
    ).astype(jnp.float32)
    return deposit(onehot, values).reshape(10, CA + 2 * HALO, H, width)


def add_rows(base, head, tail):
    k = head.shape[1]
    rows = base.shape[1]
    return jnp.concatenate(
        [base[:, :k] + head, base[:, k : rows - k], base[:, rows - k :] + tail], axis=1
    )


def selector(cells, picks):
    return (jnp.arange(cells, dtype=jnp.int32)[None, :] == jnp.array(picks, jnp.int32)[:, None]).astype(
        jnp.float32
    )


def window(raw):
    k = 2 * HALO
    center = add_rows(raw, shifted(raw[:, -k:], 1, 0), shifted(raw[:, :k], -1, 0))
    shape = center.shape
    cells = shape[3]
    flat = center.reshape(-1, cells)
    edge_cells = list(range(HALO)) + list(range(cells - HALO, cells))
    picked = jnp.einsum(
        "jn,mn->jm", selector(cells, edge_cells), flat, precision=lax.Precision.HIGHEST
    )
    right = shifted(picked[:HALO], 0, -1)
    left = shifted(picked[HALO:], 0, 1)
    edges = jnp.einsum(
        "jm,jn->mn",
        jnp.concatenate([right, left], axis=0),
        selector(cells, edge_cells),
        precision=lax.Precision.HIGHEST,
    )
    return jnp.concatenate([center, edges.reshape(shape)], axis=3)


def smooth_block(extended):
    fields = 0.25 * extended[:, :-2] + 0.5 * extended[:, 1:-1] + 0.25 * extended[:, 2:]
    fields = 0.25 * jnp.roll(fields, 1, 3) + 0.5 * fields + 0.25 * jnp.roll(fields, -1, 3)
    padded = jnp.pad(fields, ((0, 0), (0, 0), (1, 1), (0, 0)))
    return 0.25 * padded[:, :, :-2] + 0.5 * padded[:, :, 1:-1] + 0.25 * padded[:, :, 2:]


def ring_mask(extended, band_index, width, n_rad):
    lane = jnp.arange(2 * width, dtype=jnp.int32)
    columns = band_index * width + jnp.where(lane < width + width // 2, lane, lane - 2 * width)
    inside = (columns >= 0) & (columns < width * n_rad)
    return extended * inside.astype(jnp.float32)


def gradients(extended, scale_az, width):
    center = extended[:, 1:-1, :, :width]
    grad_az = (extended[:, 2:, :, :width] - extended[:, :-2, :, :width]) * scale_az
    grad_rad = (
        jnp.roll(extended[:, 1:-1], -1, 3)[..., :width] - jnp.roll(extended[:, 1:-1], 1, 3)[..., :width]
    ) * 0.5
    padded = jnp.pad(center, ((0, 0), (0, 0), (1, 1), (0, 0)))
    grad_height = (padded[:, :, 2:] - padded[:, :, :-2]) * 0.5
    return (grad_az, grad_height, grad_rad, center)


def assemble(grad_az, grad_height, grad_rad, center, recip):
    force = jnp.stack(
        [
            grad_az[3] + grad_height[6] + grad_rad[7] + 2.0 * center[7] * recip,
            grad_az[6] + grad_height[4] + grad_rad[8],
            grad_az[7] + grad_height[8] + grad_rad[5] + (center[5] - center[3]) * recip,
        ]
    )
    strain = jnp.stack(
        [
            grad_az[0] + center[2] * recip,
            grad_height[1],
            grad_rad[2],
            0.5 * (grad_height[0] + grad_az[1]),
            0.5 * (grad_rad[0] + grad_az[2] - center[0] * recip),
            0.5 * (grad_rad[1] + grad_height[2]),
        ]
    )
    return (force, strain)


def local(block_mass, block_flux, block_dest, block_count):
    sector = lax.axis_index("az")
    band_index = lax.axis_index("rad")
    n_az = lax.axis_size("az")
    n_rad = lax.axis_size("rad")
    slots = block_mass.shape[2]
    width = block_mass.shape[3]
    total_rows = CA * n_az
    start = sector * CA
    values = jnp.concatenate([block_mass[0, 0][:, None, :], block_flux[0, 0]], axis=1)
    dest = block_dest[0, 0]
    slot_index = jnp.arange(slots, dtype=jnp.int32)
    live = slot_index < block_count[0, 0]
    raw = local_rows(values, dest, live, start, total_rows, width)
    extended = window(raw)
    glob_cells = (band_index * width + jnp.arange(width, dtype=jnp.int32)).astype(jnp.float32)
    radius = width * n_rad + glob_cells + 0.5
    dtheta = 2.0 * math.pi / total_rows
    scale_az = 0.5 / (radius * dtheta)
    recip = 1.0 / radius
    smoothed_ext = smooth_block(extended)
    smoothed = smoothed_ext[:, 1:-1, :, :width]
    velocity = smoothed_ext[1:4] / (smoothed_ext[0:1] + density_base)
    combined = jnp.concatenate([velocity, smoothed_ext[4:]], axis=0)
    combined = ring_mask(combined, band_index, width, n_rad)
    grad_az, grad_height, grad_rad, center = gradients(combined, scale_az, width)
    force, strain = assemble(grad_az, grad_height, grad_rad, center, recip)
    return (smoothed, force, strain)


def solution(mesh):
    return jax.shard_map(
        local,
        mesh=mesh,
        in_specs=(
            P("az", "rad", None, None),
            P("az", "rad", None, None, None),
            P("az", "rad", None),
            P("az", "rad"),
        ),
        out_specs=(
            P(None, "az", None, "rad"),
            P(None, "az", None, "rad"),
            P(None, "az", None, "rad"),
        ),
        check_vma=False,
    )
```

```python
import math

import jax
import jax.numpy as jnp
from jax import lax
from jax.sharding import PartitionSpec as P

CA = 8
H = 32
HALO = 2


density_base = 0.5


def shifted(value, da, db):
    n_az = lax.axis_size("az")
    n_rad = lax.axis_size("rad")
    pairs = []
    for a in range(n_az):
        for b in range(n_rad):
            tb = b + db
            if 0 <= tb < n_rad:
                pairs.append((a * n_rad + b, ((a + da) % n_az) * n_rad + tb))
    shape = value.shape
    if shape[-1] % 128 == 0:
        return lax.ppermute(value, ("az", "rad"), pairs)
    dense = value.reshape(value.size // 128, 128)
    return lax.ppermute(dense, ("az", "rad"), pairs).reshape(shape)


def deposit(onehot, values):
    return jnp.einsum("ls,scn->cln", onehot, values, precision=lax.Precision.HIGHEST)


def local_rows(values, dest, live, start, total_rows, width):
    local_row = jnp.mod(dest // H - start + HALO, total_rows)
    line = local_row * H + dest % H
    onehot = (
        (jnp.arange((CA + 2 * HALO) * H, dtype=jnp.int32)[:, None] == line[None, :]) & live[None, :]
    ).astype(jnp.float32)
    return deposit(onehot, values).reshape(10, CA + 2 * HALO, H, width)


def add_rows(base, head, tail):
    k = head.shape[1]
    rows = base.shape[1]
    return jnp.concatenate(
        [base[:, :k] + head, base[:, k : rows - k], base[:, rows - k :] + tail], axis=1
    )


def selector(cells, picks):
    return (jnp.arange(cells, dtype=jnp.int32)[None, :] == jnp.array(picks, jnp.int32)[:, None]).astype(
        jnp.float32
    )


def window(raw):
    k = 2 * HALO
    shape = raw.shape
    channels, rows, height, cells = shape
    top = raw[:, :k]
    bottom = raw[:, -k:]
    edge_cells = list(range(HALO)) + list(range(cells - HALO, cells))
    picked = jnp.einsum(
        "jn,mn->jm", selector(cells, edge_cells), raw.reshape(-1, cells), precision=lax.Precision.HIGHEST
    ).reshape(2 * HALO, channels, rows * height)
    span = k * height
    head = picked[:, :, :span]
    tail = picked[:, :, -span:]

    def side(part, db):
        flat = lambda v: v.reshape(HALO, -1)
        whole = shifted(flat(part), 0, db).reshape(HALO, channels, rows * height)
        from_prev = shifted(flat(tail[part_rows[db]]), 1, db).reshape(HALO, channels, span)
        from_next = shifted(flat(head[part_rows[db]]), -1, db).reshape(HALO, channels, span)
        return jnp.concatenate(
            [whole[..., :span] + from_prev, whole[..., span:-span], whole[..., -span:] + from_next], axis=2
        )

    part_rows = {-1: slice(0, HALO), 1: slice(HALO, 2 * HALO)}
    center = add_rows(raw, shifted(bottom, 1, 0), shifted(top, -1, 0))
    right = side(picked[:HALO], -1)
    left = side(picked[HALO:], 1)
    edges = jnp.einsum(
        "jm,jn->mn",
        jnp.concatenate([right, left], axis=0).reshape(2 * HALO, -1),
        selector(cells, edge_cells),
        precision=lax.Precision.HIGHEST,
    )
    return jnp.concatenate([center, edges.reshape(shape)], axis=3)


def smooth_block(extended):
    fields = 0.25 * extended[:, :-2] + 0.5 * extended[:, 1:-1] + 0.25 * extended[:, 2:]
    fields = 0.25 * jnp.roll(fields, 1, 3) + 0.5 * fields + 0.25 * jnp.roll(fields, -1, 3)
    padded = jnp.pad(fields, ((0, 0), (0, 0), (1, 1), (0, 0)))
    return 0.25 * padded[:, :, :-2] + 0.5 * padded[:, :, 1:-1] + 0.25 * padded[:, :, 2:]


def ring_mask(extended, band_index, width, n_rad):
    lane = jnp.arange(2 * width, dtype=jnp.int32)
    columns = band_index * width + jnp.where(lane < width + width // 2, lane, lane - 2 * width)
    inside = (columns >= 0) & (columns < width * n_rad)
    return extended * inside.astype(jnp.float32)


def gradients(extended, scale_az, width):
    center = extended[:, 1:-1, :, :width]
    grad_az = (extended[:, 2:, :, :width] - extended[:, :-2, :, :width]) * scale_az
    grad_rad = (
        jnp.roll(extended[:, 1:-1], -1, 3)[..., :width] - jnp.roll(extended[:, 1:-1], 1, 3)[..., :width]
    ) * 0.5
    padded = jnp.pad(center, ((0, 0), (0, 0), (1, 1), (0, 0)))
    grad_height = (padded[:, :, 2:] - padded[:, :, :-2]) * 0.5
    return (grad_az, grad_height, grad_rad, center)


def assemble(grad_az, grad_height, grad_rad, center, recip):
    force = jnp.stack(
        [
            grad_az[3] + grad_height[6] + grad_rad[7] + 2.0 * center[7] * recip,
            grad_az[6] + grad_height[4] + grad_rad[8],
            grad_az[7] + grad_height[8] + grad_rad[5] + (center[5] - center[3]) * recip,
        ]
    )
    strain = jnp.stack(
        [
            grad_az[0] + center[2] * recip,
            grad_height[1],
            grad_rad[2],
            0.5 * (grad_height[0] + grad_az[1]),
            0.5 * (grad_rad[0] + grad_az[2] - center[0] * recip),
            0.5 * (grad_rad[1] + grad_height[2]),
        ]
    )
    return (force, strain)


def local(block_mass, block_flux, block_dest, block_count):
    sector = lax.axis_index("az")
    band_index = lax.axis_index("rad")
    n_az = lax.axis_size("az")
    n_rad = lax.axis_size("rad")
    slots = block_mass.shape[2]
    width = block_mass.shape[3]
    total_rows = CA * n_az
    start = sector * CA
    values = jnp.concatenate([block_mass[0, 0][:, None, :], block_flux[0, 0]], axis=1)
    dest = block_dest[0, 0]
    slot_index = jnp.arange(slots, dtype=jnp.int32)
    live = slot_index < block_count[0, 0]
    raw = local_rows(values, dest, live, start, total_rows, width)
    extended = window(raw)
    glob_cells = (band_index * width + jnp.arange(width, dtype=jnp.int32)).astype(jnp.float32)
    radius = width * n_rad + glob_cells + 0.5
    dtheta = 2.0 * math.pi / total_rows
    scale_az = 0.5 / (radius * dtheta)
    recip = 1.0 / radius
    smoothed_ext = smooth_block(extended)
    smoothed = smoothed_ext[:, 1:-1, :, :width]
    velocity = smoothed_ext[1:4] / (smoothed_ext[0:1] + density_base)
    combined = jnp.concatenate([velocity, smoothed_ext[4:]], axis=0)
    combined = ring_mask(combined, band_index, width, n_rad)
    grad_az, grad_height, grad_rad, center = gradients(combined, scale_az, width)
    force, strain = assemble(grad_az, grad_height, grad_rad, center, recip)
    return (smoothed, force, strain)


def solution(mesh):
    return jax.shard_map(
        local,
        mesh=mesh,
        in_specs=(
            P("az", "rad", None, None),
            P("az", "rad", None, None, None),
            P("az", "rad", None),
            P("az", "rad"),
        ),
        out_specs=(
            P(None, "az", None, "rad"),
            P(None, "az", None, "rad"),
            P(None, "az", None, "rad"),
        ),
        check_vma=False,
    )
```

```python
import math

import jax
import jax.numpy as jnp
from jax import lax
from jax.experimental import pallas as pl
from jax.experimental.pallas import tpu as pltpu
from jax.sharding import PartitionSpec as P

CA = 8
H = 32
HALO = 2


density_base = 0.5


def shifted(value, da, db):
    n_az = lax.axis_size("az")
    n_rad = lax.axis_size("rad")
    pairs = []
    for a in range(n_az):
        for b in range(n_rad):
            tb = b + db
            if 0 <= tb < n_rad:
                pairs.append((a * n_rad + b, ((a + da) % n_az) * n_rad + tb))
    shape = value.shape
    if shape[-1] % 128 == 0:
        return lax.ppermute(value, ("az", "rad"), pairs)
    dense = value.reshape(value.size // 128, 128)
    return lax.ppermute(dense, ("az", "rad"), pairs).reshape(shape)


def deposit(onehot, values):
    return jnp.einsum("ls,scn->cln", onehot, values, precision=lax.Precision.HIGHEST)


def local_rows(values, dest, live, start, total_rows, width):
    local_row = jnp.mod(dest // H - start + HALO, total_rows)
    line = local_row * H + dest % H
    onehot = (
        (jnp.arange((CA + 2 * HALO) * H, dtype=jnp.int32)[:, None] == line[None, :]) & live[None, :]
    ).astype(jnp.float32)
    return deposit(onehot, values).reshape(10, CA + 2 * HALO, H, width)


def add_rows(base, head, tail):
    k = head.shape[1]
    rows = base.shape[1]
    return jnp.concatenate(
        [base[:, :k] + head, base[:, k : rows - k], base[:, rows - k :] + tail], axis=1
    )


def selector(cells, picks):
    return (jnp.arange(cells, dtype=jnp.int32)[None, :] == jnp.array(picks, jnp.int32)[:, None]).astype(
        jnp.float32
    )


def window(raw):
    k = 2 * HALO
    center = add_rows(raw, shifted(raw[:, -k:], 1, 0), shifted(raw[:, :k], -1, 0))
    shape = center.shape
    cells = shape[3]
    flat = center.reshape(-1, cells)
    edge_cells = list(range(HALO)) + list(range(cells - HALO, cells))
    picked = jnp.einsum(
        "jn,mn->jm", selector(cells, edge_cells), flat, precision=lax.Precision.HIGHEST
    )
    right = shifted(picked[:HALO], 0, -1)
    left = shifted(picked[HALO:], 0, 1)
    edges = jnp.einsum(
        "jm,jn->mn",
        jnp.concatenate([right, left], axis=0),
        selector(cells, edge_cells),
        precision=lax.Precision.HIGHEST,
    )
    return center, edges.reshape(shape)


def smooth_block(extended):
    fields = 0.25 * extended[:, :-2] + 0.5 * extended[:, 1:-1] + 0.25 * extended[:, 2:]
    fields = 0.25 * jnp.roll(fields, 1, 3) + 0.5 * fields + 0.25 * jnp.roll(fields, -1, 3)
    padded = jnp.pad(fields, ((0, 0), (0, 0), (1, 1), (0, 0)))
    return 0.25 * padded[:, :, :-2] + 0.5 * padded[:, :, 1:-1] + 0.25 * padded[:, :, 2:]


def ring_mask(extended, band_index, width, n_rad):
    lane = jnp.arange(2 * width, dtype=jnp.int32)
    columns = band_index * width + jnp.where(lane < width + width // 2, lane, lane - 2 * width)
    inside = (columns >= 0) & (columns < width * n_rad)
    return extended * inside.astype(jnp.float32)


def gradients(extended, scale_az, width):
    center = extended[:, 1:-1, :, :width]
    grad_az = (extended[:, 2:, :, :width] - extended[:, :-2, :, :width]) * scale_az
    grad_rad = (
        jnp.roll(extended[:, 1:-1], -1, 3)[..., :width] - jnp.roll(extended[:, 1:-1], 1, 3)[..., :width]
    ) * 0.5
    padded = jnp.pad(center, ((0, 0), (0, 0), (1, 1), (0, 0)))
    grad_height = (padded[:, :, 2:] - padded[:, :, :-2]) * 0.5
    return (grad_az, grad_height, grad_rad, center)


def assemble(grad_az, grad_height, grad_rad, center, recip):
    force = jnp.stack(
        [
            grad_az[3] + grad_height[6] + grad_rad[7] + 2.0 * center[7] * recip,
            grad_az[6] + grad_height[4] + grad_rad[8],
            grad_az[7] + grad_height[8] + grad_rad[5] + (center[5] - center[3]) * recip,
        ]
    )
    strain = jnp.stack(
        [
            grad_az[0] + center[2] * recip,
            grad_height[1],
            grad_rad[2],
            0.5 * (grad_height[0] + grad_az[1]),
            0.5 * (grad_rad[0] + grad_az[2] - center[0] * recip),
            0.5 * (grad_rad[1] + grad_height[2]),
        ]
    )
    return (force, strain)


def stencil_kernel(c_ref, x_ref, scale_ref, recip_ref, xmask_ref, sm_ref, force_ref, strain_ref, sc_ref, sx_ref):
    rows, height, cells = sc_ref.shape[1:]
    lane = lax.broadcasted_iota(jnp.int32, (height, cells), 1)
    sub = lax.broadcasted_iota(jnp.int32, (height, cells), 0)

    def ring(cc, xx, shift, edge):
        rc = pltpu.roll(cc, shift, 1)
        rx = pltpu.roll(xx, shift, 1)
        return jnp.where(lane == edge, rx, rc), jnp.where(lane == edge, rc, rx)

    def below(f):
        return jnp.where(sub == 0, 0.0, pltpu.roll(f, 1, 0))

    def above(f):
        return jnp.where(sub == height - 1, 0.0, pltpu.roll(f, height - 1, 0))

    def hsmooth(f):
        return 0.25 * below(f) + 0.5 * f + 0.25 * above(f)

    def smooth_channel(c, carry):
        wc = [c_ref[c, j] for j in range(rows + 2)]
        wx = [x_ref[c, j] for j in range(rows + 2)]
        for j in range(rows):
            f1c = 0.25 * wc[j] + 0.5 * wc[j + 1] + 0.25 * wc[j + 2]
            f1x = 0.25 * wx[j] + 0.5 * wx[j + 1] + 0.25 * wx[j + 2]
            pc, px = ring(f1c, f1x, 1, 0)
            nc, nx = ring(f1c, f1x, cells - 1, cells - 1)
            sc_ref[c, j] = hsmooth(0.25 * pc + 0.5 * f1c + 0.25 * nc)
            sx_ref[c, j] = hsmooth(0.25 * px + 0.5 * f1x + 0.25 * nx)
        return carry

    lax.fori_loop(0, sc_ref.shape[0], smooth_channel, 0)
    scale = scale_ref[...]
    recip = recip_ref[...]
    xmask = xmask_ref[...]

    def comb(ref, j, k):
        if k < 3:
            return ref[k + 1, j] / (ref[0, j] + density_base)
        return ref[k + 1, j]

    def out_row(r, carry):
        for c in range(sm_ref.shape[0]):
            sm_ref[c, r] = sc_ref[c, r + 1]
        center = [comb(sc_ref, r + 1, k) for k in range(9)]
        grad_az = {}
        for k in (0, 1, 2, 3, 6, 7):
            grad_az[k] = (comb(sc_ref, r + 2, k) - comb(sc_ref, r, k)) * scale
        grad_height = {k: (above(center[k]) - below(center[k])) * 0.5 for k in (0, 1, 2, 4, 6, 8)}
        grad_rad = {}
        for k in (0, 1, 2, 5, 7, 8):
            edge = comb(sx_ref, r + 1, k) * xmask
            pc, _ = ring(center[k], edge, 1, 0)
            nc, _ = ring(center[k], edge, cells - 1, cells - 1)
            grad_rad[k] = (nc - pc) * 0.5
        force_ref[0, r] = grad_az[3] + grad_height[6] + grad_rad[7] + 2.0 * center[7] * recip
        force_ref[1, r] = grad_az[6] + grad_height[4] + grad_rad[8]
        force_ref[2, r] = grad_az[7] + grad_height[8] + grad_rad[5] + (center[5] - center[3]) * recip
        strain_ref[0, r] = grad_az[0] + center[2] * recip
        strain_ref[1, r] = grad_height[1]
        strain_ref[2, r] = grad_rad[2]
        strain_ref[3, r] = 0.5 * (grad_height[0] + grad_az[1])
        strain_ref[4, r] = 0.5 * (grad_rad[0] + grad_az[2] - center[0] * recip)
        strain_ref[5, r] = 0.5 * (grad_rad[1] + grad_height[2])
        return carry

    lax.fori_loop(0, sm_ref.shape[1], out_row, 0)


def stencil(center, edges, scale_az, recip, xmask):
    channels, rows, height, cells = center.shape
    own = rows - 2 * HALO
    vmem = pl.BlockSpec(memory_space=pltpu.VMEM)
    shape = lambda n: jax.ShapeDtypeStruct((n, own, height, cells), jnp.float32)
    return pl.pallas_call(
        stencil_kernel,
        out_shape=(shape(channels), shape(3), shape(6)),
        in_specs=[vmem] * 5,
        out_specs=(vmem, vmem, vmem),
        scratch_shapes=[pltpu.VMEM((channels, rows - 2, height, cells), jnp.float32)] * 2,
    )(center, edges, scale_az.reshape(1, cells), recip.reshape(1, cells), xmask.reshape(1, cells))


def local(block_mass, block_flux, block_dest, block_count):
    sector = lax.axis_index("az")
    band_index = lax.axis_index("rad")
    n_az = lax.axis_size("az")
    n_rad = lax.axis_size("rad")
    slots = block_mass.shape[2]
    width = block_mass.shape[3]
    total_rows = CA * n_az
    start = sector * CA
    values = jnp.concatenate([block_mass[0, 0][:, None, :], block_flux[0, 0]], axis=1)
    dest = block_dest[0, 0]
    slot_index = jnp.arange(slots, dtype=jnp.int32)
    live = slot_index < block_count[0, 0]
    raw = local_rows(values, dest, live, start, total_rows, width)
    center, edges = window(raw)
    glob_cells = (band_index * width + jnp.arange(width, dtype=jnp.int32)).astype(jnp.float32)
    radius = width * n_rad + glob_cells + 0.5
    dtheta = 2.0 * math.pi / total_rows
    scale_az = 0.5 / (radius * dtheta)
    recip = 1.0 / radius
    xmask = ring_mask(jnp.ones((2 * width,), jnp.float32), band_index, width, n_rad)[width:]
    return stencil(center, edges, scale_az, recip, xmask)


def solution(mesh):
    return jax.shard_map(
        local,
        mesh=mesh,
        in_specs=(
            P("az", "rad", None, None),
            P("az", "rad", None, None, None),
            P("az", "rad", None),
            P("az", "rad"),
        ),
        out_specs=(
            P(None, "az", None, "rad"),
            P(None, "az", None, "rad"),
            P(None, "az", None, "rad"),
        ),
        check_vma=False,
    )
```

```python
import math

import jax
import jax.numpy as jnp
from jax import lax
from jax.experimental import pallas as pl
from jax.experimental.pallas import tpu as pltpu
from jax.sharding import PartitionSpec as P

CA = 8
H = 32
HALO = 2


density_base = 0.5


def shifted(value, da, db):
    n_az = lax.axis_size("az")
    n_rad = lax.axis_size("rad")
    pairs = []
    for a in range(n_az):
        for b in range(n_rad):
            tb = b + db
            if 0 <= tb < n_rad:
                pairs.append((a * n_rad + b, ((a + da) % n_az) * n_rad + tb))
    shape = value.shape
    if shape[-1] % 128 == 0:
        return lax.ppermute(value, ("az", "rad"), pairs)
    dense = value.reshape(value.size // 128, 128)
    return lax.ppermute(dense, ("az", "rad"), pairs).reshape(shape)


def deposit(onehot, values):
    return jnp.einsum("ls,scn->cln", onehot, values, precision=lax.Precision.HIGHEST)


def local_rows(values, dest, live, start, total_rows, width, lines):
    local_row = jnp.mod(dest // H - start + HALO, total_rows)
    line = local_row * H + dest % H
    onehot = ((lines[:, None] == line[None, :]) & live[None, :]).astype(jnp.float32)
    return deposit(onehot, values).reshape(10, -1, H, width)


def add_rows(base, head, tail):
    k = head.shape[1]
    rows = base.shape[1]
    return jnp.concatenate(
        [base[:, :k] + head, base[:, k : rows - k], base[:, rows - k :] + tail], axis=1
    )


def selector(cells, picks):
    return (jnp.arange(cells, dtype=jnp.int32)[None, :] == jnp.array(picks, jnp.int32)[:, None]).astype(
        jnp.float32
    )


def window(outer, inner):
    k = 2 * HALO
    top = outer[:, :k]
    bottom = outer[:, k:]
    from_prev = shifted(bottom, 1, 0)
    from_next = shifted(top, -1, 0)
    center = jnp.concatenate([top + from_prev, inner(), bottom + from_next], axis=1)
    shape = center.shape
    cells = shape[3]
    flat = center.reshape(-1, cells)
    edge_cells = list(range(HALO)) + list(range(cells - HALO, cells))
    picked = jnp.einsum(
        "jn,mn->jm", selector(cells, edge_cells), flat, precision=lax.Precision.HIGHEST
    )
    right = shifted(picked[:HALO], 0, -1)
    left = shifted(picked[HALO:], 0, 1)
    edges = jnp.einsum(
        "jm,jn->mn",
        jnp.concatenate([right, left], axis=0),
        selector(cells, edge_cells),
        precision=lax.Precision.HIGHEST,
    )
    return center, edges.reshape(shape)


def smooth_block(extended):
    fields = 0.25 * extended[:, :-2] + 0.5 * extended[:, 1:-1] + 0.25 * extended[:, 2:]
    fields = 0.25 * jnp.roll(fields, 1, 3) + 0.5 * fields + 0.25 * jnp.roll(fields, -1, 3)
    padded = jnp.pad(fields, ((0, 0), (0, 0), (1, 1), (0, 0)))
    return 0.25 * padded[:, :, :-2] + 0.5 * padded[:, :, 1:-1] + 0.25 * padded[:, :, 2:]


def ring_mask(extended, band_index, width, n_rad):
    lane = jnp.arange(2 * width, dtype=jnp.int32)
    columns = band_index * width + jnp.where(lane < width + width // 2, lane, lane - 2 * width)
    inside = (columns >= 0) & (columns < width * n_rad)
    return extended * inside.astype(jnp.float32)


def gradients(extended, scale_az, width):
    center = extended[:, 1:-1, :, :width]
    grad_az = (extended[:, 2:, :, :width] - extended[:, :-2, :, :width]) * scale_az
    grad_rad = (
        jnp.roll(extended[:, 1:-1], -1, 3)[..., :width] - jnp.roll(extended[:, 1:-1], 1, 3)[..., :width]
    ) * 0.5
    padded = jnp.pad(center, ((0, 0), (0, 0), (1, 1), (0, 0)))
    grad_height = (padded[:, :, 2:] - padded[:, :, :-2]) * 0.5
    return (grad_az, grad_height, grad_rad, center)


def assemble(grad_az, grad_height, grad_rad, center, recip):
    force = jnp.stack(
        [
            grad_az[3] + grad_height[6] + grad_rad[7] + 2.0 * center[7] * recip,
            grad_az[6] + grad_height[4] + grad_rad[8],
            grad_az[7] + grad_height[8] + grad_rad[5] + (center[5] - center[3]) * recip,
        ]
    )
    strain = jnp.stack(
        [
            grad_az[0] + center[2] * recip,
            grad_height[1],
            grad_rad[2],
            0.5 * (grad_height[0] + grad_az[1]),
            0.5 * (grad_rad[0] + grad_az[2] - center[0] * recip),
            0.5 * (grad_rad[1] + grad_height[2]),
        ]
    )
    return (force, strain)


def stencil_kernel(c_ref, x_ref, scale_ref, recip_ref, xmask_ref, sm_ref, force_ref, strain_ref, sc_ref, sx_ref):
    rows, height, cells = sc_ref.shape[1:]
    lane = lax.broadcasted_iota(jnp.int32, (height, cells), 1)
    sub = lax.broadcasted_iota(jnp.int32, (height, cells), 0)

    def ring(cc, xx, shift, edge):
        rc = pltpu.roll(cc, shift, 1)
        rx = pltpu.roll(xx, shift, 1)
        return jnp.where(lane == edge, rx, rc), jnp.where(lane == edge, rc, rx)

    def below(f):
        return jnp.where(sub == 0, 0.0, pltpu.roll(f, 1, 0))

    def above(f):
        return jnp.where(sub == height - 1, 0.0, pltpu.roll(f, height - 1, 0))

    def hsmooth(f):
        return 0.25 * below(f) + 0.5 * f + 0.25 * above(f)

    def smooth_channel(c, carry):
        wc = [c_ref[c, j] for j in range(rows + 2)]
        wx = [x_ref[c, j] for j in range(rows + 2)]
        for j in range(rows):
            f1c = 0.25 * wc[j] + 0.5 * wc[j + 1] + 0.25 * wc[j + 2]
            f1x = 0.25 * wx[j] + 0.5 * wx[j + 1] + 0.25 * wx[j + 2]
            pc, px = ring(f1c, f1x, 1, 0)
            nc, nx = ring(f1c, f1x, cells - 1, cells - 1)
            sc_ref[c, j] = hsmooth(0.25 * pc + 0.5 * f1c + 0.25 * nc)
            sx_ref[c, j] = hsmooth(0.25 * px + 0.5 * f1x + 0.25 * nx)
        return carry

    lax.fori_loop(0, sc_ref.shape[0], smooth_channel, 0)
    scale = scale_ref[...]
    recip = recip_ref[...]
    xmask = xmask_ref[...]

    def comb(ref, j, k):
        if k < 3:
            return ref[k + 1, j] / (ref[0, j] + density_base)
        return ref[k + 1, j]

    def out_row(r, carry):
        for c in range(sm_ref.shape[0]):
            sm_ref[c, r] = sc_ref[c, r + 1]
        center = [comb(sc_ref, r + 1, k) for k in range(9)]
        grad_az = {}
        for k in (0, 1, 2, 3, 6, 7):
            grad_az[k] = (comb(sc_ref, r + 2, k) - comb(sc_ref, r, k)) * scale
        grad_height = {k: (above(center[k]) - below(center[k])) * 0.5 for k in (0, 1, 2, 4, 6, 8)}
        grad_rad = {}
        for k in (0, 1, 2, 5, 7, 8):
            edge = comb(sx_ref, r + 1, k) * xmask
            pc, _ = ring(center[k], edge, 1, 0)
            nc, _ = ring(center[k], edge, cells - 1, cells - 1)
            grad_rad[k] = (nc - pc) * 0.5
        force_ref[0, r] = grad_az[3] + grad_height[6] + grad_rad[7] + 2.0 * center[7] * recip
        force_ref[1, r] = grad_az[6] + grad_height[4] + grad_rad[8]
        force_ref[2, r] = grad_az[7] + grad_height[8] + grad_rad[5] + (center[5] - center[3]) * recip
        strain_ref[0, r] = grad_az[0] + center[2] * recip
        strain_ref[1, r] = grad_height[1]
        strain_ref[2, r] = grad_rad[2]
        strain_ref[3, r] = 0.5 * (grad_height[0] + grad_az[1])
        strain_ref[4, r] = 0.5 * (grad_rad[0] + grad_az[2] - center[0] * recip)
        strain_ref[5, r] = 0.5 * (grad_rad[1] + grad_height[2])
        return carry

    lax.fori_loop(0, sm_ref.shape[1], out_row, 0)


def stencil(center, edges, scale_az, recip, xmask):
    channels, rows, height, cells = center.shape
    own = rows - 2 * HALO
    vmem = pl.BlockSpec(memory_space=pltpu.VMEM)
    shape = lambda n: jax.ShapeDtypeStruct((n, own, height, cells), jnp.float32)
    return pl.pallas_call(
        stencil_kernel,
        out_shape=(shape(channels), shape(3), shape(6)),
        in_specs=[vmem] * 5,
        out_specs=(vmem, vmem, vmem),
        scratch_shapes=[pltpu.VMEM((channels, rows - 2, height, cells), jnp.float32)] * 2,
    )(center, edges, scale_az.reshape(1, cells), recip.reshape(1, cells), xmask.reshape(1, cells))


def local(block_mass, block_flux, block_dest, block_count):
    sector = lax.axis_index("az")
    band_index = lax.axis_index("rad")
    n_az = lax.axis_size("az")
    n_rad = lax.axis_size("rad")
    slots = block_mass.shape[2]
    width = block_mass.shape[3]
    total_rows = CA * n_az
    start = sector * CA
    values = jnp.concatenate([block_mass[0, 0][:, None, :], block_flux[0, 0]], axis=1)
    dest = block_dest[0, 0]
    slot_index = jnp.arange(slots, dtype=jnp.int32)
    live = slot_index < block_count[0, 0]
    k = 2 * HALO * H
    lines = jnp.arange((CA + 2 * HALO) * H, dtype=jnp.int32)
    outer = local_rows(values, dest, live, start, total_rows, width, jnp.concatenate([lines[:k], lines[-k:]]))
    inner = lambda: local_rows(values, dest, live, start, total_rows, width, lines[k:-k])
    center, edges = window(outer, inner)
    glob_cells = (band_index * width + jnp.arange(width, dtype=jnp.int32)).astype(jnp.float32)
    radius = width * n_rad + glob_cells + 0.5
    dtheta = 2.0 * math.pi / total_rows
    scale_az = 0.5 / (radius * dtheta)
    recip = 1.0 / radius
    xmask = ring_mask(jnp.ones((2 * width,), jnp.float32), band_index, width, n_rad)[width:]
    return stencil(center, edges, scale_az, recip, xmask)


def solution(mesh):
    return jax.shard_map(
        local,
        mesh=mesh,
        in_specs=(
            P("az", "rad", None, None),
            P("az", "rad", None, None, None),
            P("az", "rad", None),
            P("az", "rad"),
        ),
        out_specs=(
            P(None, "az", None, "rad"),
            P(None, "az", None, "rad"),
            P(None, "az", None, "rad"),
        ),
        check_vma=False,
    )
```

```python
import math

import jax
import jax.numpy as jnp
from jax import lax
from jax.experimental import pallas as pl
from jax.experimental.pallas import tpu as pltpu
from jax.sharding import PartitionSpec as P

CA = 8
H = 32
HALO = 2


density_base = 0.5


def shifted(value, da, db):
    n_az = lax.axis_size("az")
    n_rad = lax.axis_size("rad")
    pairs = []
    for a in range(n_az):
        for b in range(n_rad):
            tb = b + db
            if 0 <= tb < n_rad:
                pairs.append((a * n_rad + b, ((a + da) % n_az) * n_rad + tb))
    shape = value.shape
    if shape[-1] % 128 == 0:
        return lax.ppermute(value, ("az", "rad"), pairs)
    dense = value.reshape(value.size // 128, 128)
    return lax.ppermute(dense, ("az", "rad"), pairs).reshape(shape)


def deposit(onehot, values):
    out = jnp.einsum("ls,scn->lcn", onehot, values, precision=lax.Precision.HIGHEST)
    return jnp.transpose(out, (1, 0, 2))


def local_rows(values, dest, live, start, total_rows, width):
    local_row = jnp.mod(dest // H - start + HALO, total_rows)
    line = local_row * H + dest % H
    onehot = (
        (jnp.arange((CA + 2 * HALO) * H, dtype=jnp.int32)[:, None] == line[None, :]) & live[None, :]
    ).astype(jnp.float32)
    return deposit(onehot, values).reshape(10, CA + 2 * HALO, H, width)


def add_rows(base, head, tail):
    k = head.shape[1]
    rows = base.shape[1]
    return jnp.concatenate(
        [base[:, :k] + head, base[:, k : rows - k], base[:, rows - k :] + tail], axis=1
    )


def selector(cells, picks):
    return (jnp.arange(cells, dtype=jnp.int32)[None, :] == jnp.array(picks, jnp.int32)[:, None]).astype(
        jnp.float32
    )


def window(raw):
    k = 2 * HALO
    center = add_rows(raw, shifted(raw[:, -k:], 1, 0), shifted(raw[:, :k], -1, 0))
    shape = center.shape
    cells = shape[3]
    flat = center.reshape(-1, cells)
    edge_cells = list(range(HALO)) + list(range(cells - HALO, cells))
    picked = jnp.einsum(
        "jn,mn->jm", selector(cells, edge_cells), flat, precision=lax.Precision.HIGHEST
    )
    right = shifted(picked[:HALO], 0, -1)
    left = shifted(picked[HALO:], 0, 1)
    edges = jnp.einsum(
        "jm,jn->mn",
        jnp.concatenate([right, left], axis=0),
        selector(cells, edge_cells),
        precision=lax.Precision.HIGHEST,
    )
    return center, edges.reshape(shape)


def smooth_block(extended):
    fields = 0.25 * extended[:, :-2] + 0.5 * extended[:, 1:-1] + 0.25 * extended[:, 2:]
    fields = 0.25 * jnp.roll(fields, 1, 3) + 0.5 * fields + 0.25 * jnp.roll(fields, -1, 3)
    padded = jnp.pad(fields, ((0, 0), (0, 0), (1, 1), (0, 0)))
    return 0.25 * padded[:, :, :-2] + 0.5 * padded[:, :, 1:-1] + 0.25 * padded[:, :, 2:]


def ring_mask(extended, band_index, width, n_rad):
    lane = jnp.arange(2 * width, dtype=jnp.int32)
    columns = band_index * width + jnp.where(lane < width + width // 2, lane, lane - 2 * width)
    inside = (columns >= 0) & (columns < width * n_rad)
    return extended * inside.astype(jnp.float32)


def gradients(extended, scale_az, width):
    center = extended[:, 1:-1, :, :width]
    grad_az = (extended[:, 2:, :, :width] - extended[:, :-2, :, :width]) * scale_az
    grad_rad = (
        jnp.roll(extended[:, 1:-1], -1, 3)[..., :width] - jnp.roll(extended[:, 1:-1], 1, 3)[..., :width]
    ) * 0.5
    padded = jnp.pad(center, ((0, 0), (0, 0), (1, 1), (0, 0)))
    grad_height = (padded[:, :, 2:] - padded[:, :, :-2]) * 0.5
    return (grad_az, grad_height, grad_rad, center)


def assemble(grad_az, grad_height, grad_rad, center, recip):
    force = jnp.stack(
        [
            grad_az[3] + grad_height[6] + grad_rad[7] + 2.0 * center[7] * recip,
            grad_az[6] + grad_height[4] + grad_rad[8],
            grad_az[7] + grad_height[8] + grad_rad[5] + (center[5] - center[3]) * recip,
        ]
    )
    strain = jnp.stack(
        [
            grad_az[0] + center[2] * recip,
            grad_height[1],
            grad_rad[2],
            0.5 * (grad_height[0] + grad_az[1]),
            0.5 * (grad_rad[0] + grad_az[2] - center[0] * recip),
            0.5 * (grad_rad[1] + grad_height[2]),
        ]
    )
    return (force, strain)


def stencil_kernel(c_ref, x_ref, scale_ref, recip_ref, xmask_ref, sm_ref, force_ref, strain_ref, sc_ref, sx_ref):
    rows, height, cells = sc_ref.shape[1:]
    lane = lax.broadcasted_iota(jnp.int32, (height, cells), 1)
    sub = lax.broadcasted_iota(jnp.int32, (height, cells), 0)

    def ring(cc, xx, shift, edge):
        rc = pltpu.roll(cc, shift, 1)
        rx = pltpu.roll(xx, shift, 1)
        return jnp.where(lane == edge, rx, rc), jnp.where(lane == edge, rc, rx)

    def below(f):
        return jnp.where(sub == 0, 0.0, pltpu.roll(f, 1, 0))

    def above(f):
        return jnp.where(sub == height - 1, 0.0, pltpu.roll(f, height - 1, 0))

    def hsmooth(f):
        return 0.25 * below(f) + 0.5 * f + 0.25 * above(f)

    def smooth_channel(c, carry):
        wc = [c_ref[c, j] for j in range(rows + 2)]
        wx = [x_ref[c, j] for j in range(rows + 2)]
        for j in range(rows):
            f1c = 0.25 * wc[j] + 0.5 * wc[j + 1] + 0.25 * wc[j + 2]
            f1x = 0.25 * wx[j] + 0.5 * wx[j + 1] + 0.25 * wx[j + 2]
            pc, px = ring(f1c, f1x, 1, 0)
            nc, nx = ring(f1c, f1x, cells - 1, cells - 1)
            sc_ref[c, j] = hsmooth(0.25 * pc + 0.5 * f1c + 0.25 * nc)
            sx_ref[c, j] = hsmooth(0.25 * px + 0.5 * f1x + 0.25 * nx)
        return carry

    lax.fori_loop(0, sc_ref.shape[0], smooth_channel, 0)
    scale = scale_ref[...]
    recip = recip_ref[...]
    xmask = xmask_ref[...]

    def comb(ref, j, k):
        if k < 3:
            return ref[k + 1, j] / (ref[0, j] + density_base)
        return ref[k + 1, j]

    def out_row(r, carry):
        for c in range(sm_ref.shape[0]):
            sm_ref[c, r] = sc_ref[c, r + 1]
        center = [comb(sc_ref, r + 1, k) for k in range(9)]
        grad_az = {}
        for k in (0, 1, 2, 3, 6, 7):
            grad_az[k] = (comb(sc_ref, r + 2, k) - comb(sc_ref, r, k)) * scale
        grad_height = {k: (above(center[k]) - below(center[k])) * 0.5 for k in (0, 1, 2, 4, 6, 8)}
        grad_rad = {}
        for k in (0, 1, 2, 5, 7, 8):
            edge = comb(sx_ref, r + 1, k) * xmask
            pc, _ = ring(center[k], edge, 1, 0)
            nc, _ = ring(center[k], edge, cells - 1, cells - 1)
            grad_rad[k] = (nc - pc) * 0.5
        force_ref[0, r] = grad_az[3] + grad_height[6] + grad_rad[7] + 2.0 * center[7] * recip
        force_ref[1, r] = grad_az[6] + grad_height[4] + grad_rad[8]
        force_ref[2, r] = grad_az[7] + grad_height[8] + grad_rad[5] + (center[5] - center[3]) * recip
        strain_ref[0, r] = grad_az[0] + center[2] * recip
        strain_ref[1, r] = grad_height[1]
        strain_ref[2, r] = grad_rad[2]
        strain_ref[3, r] = 0.5 * (grad_height[0] + grad_az[1])
        strain_ref[4, r] = 0.5 * (grad_rad[0] + grad_az[2] - center[0] * recip)
        strain_ref[5, r] = 0.5 * (grad_rad[1] + grad_height[2])
        return carry

    lax.fori_loop(0, sm_ref.shape[1], out_row, 0)


def stencil(center, edges, scale_az, recip, xmask):
    channels, rows, height, cells = center.shape
    own = rows - 2 * HALO
    vmem = pl.BlockSpec(memory_space=pltpu.VMEM)
    shape = lambda n: jax.ShapeDtypeStruct((n, own, height, cells), jnp.float32)
    return pl.pallas_call(
        stencil_kernel,
        out_shape=(shape(channels), shape(3), shape(6)),
        in_specs=[vmem] * 5,
        out_specs=(vmem, vmem, vmem),
        scratch_shapes=[pltpu.VMEM((channels, rows - 2, height, cells), jnp.float32)] * 2,
    )(center, edges, scale_az.reshape(1, cells), recip.reshape(1, cells), xmask.reshape(1, cells))


def local(block_mass, block_flux, block_dest, block_count):
    sector = lax.axis_index("az")
    band_index = lax.axis_index("rad")
    n_az = lax.axis_size("az")
    n_rad = lax.axis_size("rad")
    slots = block_mass.shape[2]
    width = block_mass.shape[3]
    total_rows = CA * n_az
    start = sector * CA
    values = jnp.concatenate([block_mass[0, 0][:, None, :], block_flux[0, 0]], axis=1)
    dest = block_dest[0, 0]
    slot_index = jnp.arange(slots, dtype=jnp.int32)
    live = slot_index < block_count[0, 0]
    raw = local_rows(values, dest, live, start, total_rows, width)
    center, edges = window(raw)
    glob_cells = (band_index * width + jnp.arange(width, dtype=jnp.int32)).astype(jnp.float32)
    radius = width * n_rad + glob_cells + 0.5
    dtheta = 2.0 * math.pi / total_rows
    scale_az = 0.5 / (radius * dtheta)
    recip = 1.0 / radius
    xmask = ring_mask(jnp.ones((2 * width,), jnp.float32), band_index, width, n_rad)[width:]
    return stencil(center, edges, scale_az, recip, xmask)


def solution(mesh):
    return jax.shard_map(
        local,
        mesh=mesh,
        in_specs=(
            P("az", "rad", None, None),
            P("az", "rad", None, None, None),
            P("az", "rad", None),
            P("az", "rad"),
        ),
        out_specs=(
            P(None, "az", None, "rad"),
            P(None, "az", None, "rad"),
            P(None, "az", None, "rad"),
        ),
        check_vma=False,
    )
```

```python
import math

import jax
import jax.numpy as jnp
from jax import lax
from jax.experimental import pallas as pl
from jax.experimental.pallas import tpu as pltpu
from jax.sharding import PartitionSpec as P

CA = 8
H = 32
HALO = 2


density_base = 0.5


def shifted(value, da, db):
    n_az = lax.axis_size("az")
    n_rad = lax.axis_size("rad")
    pairs = []
    for a in range(n_az):
        for b in range(n_rad):
            tb = b + db
            if 0 <= tb < n_rad:
                pairs.append((a * n_rad + b, ((a + da) % n_az) * n_rad + tb))
    shape = value.shape
    if shape[-1] % 128 == 0:
        return lax.ppermute(value, ("az", "rad"), pairs)
    dense = value.reshape(value.size // 128, 128)
    return lax.ppermute(dense, ("az", "rad"), pairs).reshape(shape)


def deposit(onehot, values):
    out = jnp.einsum("ls,scn->lcn", onehot, values, precision=lax.Precision.HIGHEST)
    return jnp.transpose(out, (1, 0, 2))


def local_rows(values, dest, live, start, total_rows, width):
    local_row = jnp.mod(dest // H - start + HALO, total_rows)
    line = local_row * H + dest % H
    onehot = (
        (jnp.arange((CA + 2 * HALO) * H, dtype=jnp.int32)[:, None] == line[None, :]) & live[None, :]
    ).astype(jnp.float32)
    return deposit(onehot, values).reshape(10, CA + 2 * HALO, H, width)


def add_rows(base, head, tail):
    k = head.shape[1]
    rows = base.shape[1]
    return jnp.concatenate(
        [base[:, :k] + head, base[:, k : rows - k], base[:, rows - k :] + tail], axis=1
    )


def selector(cells, picks):
    return (jnp.arange(cells, dtype=jnp.int32)[None, :] == jnp.array(picks, jnp.int32)[:, None]).astype(
        jnp.float32
    )


def window(raw):
    k = 2 * HALO
    center = add_rows(raw, shifted(raw[:, -k:], 1, 0), shifted(raw[:, :k], -1, 0))
    shape = center.shape
    cells = shape[3]
    flat = center.reshape(-1, cells)
    edge_cells = list(range(HALO)) + list(range(cells - HALO, cells))
    picked = jnp.einsum(
        "jn,mn->jm", selector(cells, edge_cells), flat, precision=lax.Precision.HIGHEST
    )
    right = shifted(picked[:HALO], 0, -1)
    left = shifted(picked[HALO:], 0, 1)
    edges = jnp.einsum(
        "jm,jn->mn",
        jnp.concatenate([right, left], axis=0),
        selector(cells, edge_cells),
        precision=lax.Precision.HIGHEST,
    )
    return center, edges.reshape(shape)


def smooth_block(extended):
    fields = 0.25 * extended[:, :-2] + 0.5 * extended[:, 1:-1] + 0.25 * extended[:, 2:]
    fields = 0.25 * jnp.roll(fields, 1, 3) + 0.5 * fields + 0.25 * jnp.roll(fields, -1, 3)
    padded = jnp.pad(fields, ((0, 0), (0, 0), (1, 1), (0, 0)))
    return 0.25 * padded[:, :, :-2] + 0.5 * padded[:, :, 1:-1] + 0.25 * padded[:, :, 2:]


def ring_mask(extended, band_index, width, n_rad):
    lane = jnp.arange(2 * width, dtype=jnp.int32)
    columns = band_index * width + jnp.where(lane < width + width // 2, lane, lane - 2 * width)
    inside = (columns >= 0) & (columns < width * n_rad)
    return extended * inside.astype(jnp.float32)


def gradients(extended, scale_az, width):
    center = extended[:, 1:-1, :, :width]
    grad_az = (extended[:, 2:, :, :width] - extended[:, :-2, :, :width]) * scale_az
    grad_rad = (
        jnp.roll(extended[:, 1:-1], -1, 3)[..., :width] - jnp.roll(extended[:, 1:-1], 1, 3)[..., :width]
    ) * 0.5
    padded = jnp.pad(center, ((0, 0), (0, 0), (1, 1), (0, 0)))
    grad_height = (padded[:, :, 2:] - padded[:, :, :-2]) * 0.5
    return (grad_az, grad_height, grad_rad, center)


def assemble(grad_az, grad_height, grad_rad, center, recip):
    force = jnp.stack(
        [
            grad_az[3] + grad_height[6] + grad_rad[7] + 2.0 * center[7] * recip,
            grad_az[6] + grad_height[4] + grad_rad[8],
            grad_az[7] + grad_height[8] + grad_rad[5] + (center[5] - center[3]) * recip,
        ]
    )
    strain = jnp.stack(
        [
            grad_az[0] + center[2] * recip,
            grad_height[1],
            grad_rad[2],
            0.5 * (grad_height[0] + grad_az[1]),
            0.5 * (grad_rad[0] + grad_az[2] - center[0] * recip),
            0.5 * (grad_rad[1] + grad_height[2]),
        ]
    )
    return (force, strain)


def stencil_kernel(
    c_ref, x_ref, scale_ref, recip_ref, xmask_ref, sm_ref, force_ref, strain_ref, sc_ref, sx_ref, cc_ref, cx_ref
):
    rows, height, cells = sc_ref.shape[1:]
    lane = lax.broadcasted_iota(jnp.int32, (height, cells), 1)
    sub = lax.broadcasted_iota(jnp.int32, (height, cells), 0)

    def ring(cc, xx, shift, edge):
        rc = pltpu.roll(cc, shift, 1)
        rx = pltpu.roll(xx, shift, 1)
        return jnp.where(lane == edge, rx, rc), jnp.where(lane == edge, rc, rx)

    def below(f):
        return jnp.where(sub == 0, 0.0, pltpu.roll(f, 1, 0))

    def above(f):
        return jnp.where(sub == height - 1, 0.0, pltpu.roll(f, height - 1, 0))

    def hsmooth(f):
        return 0.25 * below(f) + 0.5 * f + 0.25 * above(f)

    def smooth_channel(c, carry):
        wc = [c_ref[c, j] for j in range(rows + 2)]
        wx = [x_ref[c, j] for j in range(rows + 2)]
        for j in range(rows):
            f1c = 0.25 * wc[j] + 0.5 * wc[j + 1] + 0.25 * wc[j + 2]
            f1x = 0.25 * wx[j] + 0.5 * wx[j + 1] + 0.25 * wx[j + 2]
            pc, px = ring(f1c, f1x, 1, 0)
            nc, nx = ring(f1c, f1x, cells - 1, cells - 1)
            sc_ref[c, j] = hsmooth(0.25 * pc + 0.5 * f1c + 0.25 * nc)
            sx_ref[c, j] = hsmooth(0.25 * px + 0.5 * f1x + 0.25 * nx)
        return carry

    lax.fori_loop(0, sc_ref.shape[0], smooth_channel, 0)
    scale = scale_ref[...]
    recip = recip_ref[...]
    xmask = xmask_ref[...]

    def combine_row(j, carry):
        dc = sc_ref[0, j] + density_base
        dx = sx_ref[0, j] + density_base
        for k in range(cc_ref.shape[0]):
            if k < 3:
                cc_ref[k, j] = sc_ref[k + 1, j] / dc
                cx_ref[k, j] = sx_ref[k + 1, j] / dx * xmask
            else:
                cc_ref[k, j] = sc_ref[k + 1, j]
                cx_ref[k, j] = sx_ref[k + 1, j] * xmask
        return carry

    lax.fori_loop(0, rows, combine_row, 0)

    def out_row(r, carry):
        for c in range(sm_ref.shape[0]):
            sm_ref[c, r] = sc_ref[c, r + 1]
        center = [cc_ref[k, r + 1] for k in range(cc_ref.shape[0])]
        grad_az = {k: (cc_ref[k, r + 2] - cc_ref[k, r]) * scale for k in (0, 1, 2, 3, 6, 7)}
        grad_height = {k: (above(center[k]) - below(center[k])) * 0.5 for k in (0, 1, 2, 4, 6, 8)}
        grad_rad = {}
        for k in (0, 1, 2, 5, 7, 8):
            edge = cx_ref[k, r + 1]
            pc, _ = ring(center[k], edge, 1, 0)
            nc, _ = ring(center[k], edge, cells - 1, cells - 1)
            grad_rad[k] = (nc - pc) * 0.5
        force_ref[0, r] = grad_az[3] + grad_height[6] + grad_rad[7] + 2.0 * center[7] * recip
        force_ref[1, r] = grad_az[6] + grad_height[4] + grad_rad[8]
        force_ref[2, r] = grad_az[7] + grad_height[8] + grad_rad[5] + (center[5] - center[3]) * recip
        strain_ref[0, r] = grad_az[0] + center[2] * recip
        strain_ref[1, r] = grad_height[1]
        strain_ref[2, r] = grad_rad[2]
        strain_ref[3, r] = 0.5 * (grad_height[0] + grad_az[1])
        strain_ref[4, r] = 0.5 * (grad_rad[0] + grad_az[2] - center[0] * recip)
        strain_ref[5, r] = 0.5 * (grad_rad[1] + grad_height[2])
        return carry

    lax.fori_loop(0, sm_ref.shape[1], out_row, 0)


def stencil(center, edges, scale_az, recip, xmask):
    channels, rows, height, cells = center.shape
    own = rows - 2 * HALO
    vmem = pl.BlockSpec(memory_space=pltpu.VMEM)
    shape = lambda n: jax.ShapeDtypeStruct((n, own, height, cells), jnp.float32)
    scratch = lambda n: pltpu.VMEM((n, rows - 2, height, cells), jnp.float32)
    return pl.pallas_call(
        stencil_kernel,
        out_shape=(shape(channels), shape(3), shape(6)),
        in_specs=[vmem] * 5,
        out_specs=(vmem, vmem, vmem),
        scratch_shapes=[scratch(channels), scratch(channels), scratch(channels - 1), scratch(channels - 1)],
    )(center, edges, scale_az.reshape(1, cells), recip.reshape(1, cells), xmask.reshape(1, cells))


def local(block_mass, block_flux, block_dest, block_count):
    sector = lax.axis_index("az")
    band_index = lax.axis_index("rad")
    n_az = lax.axis_size("az")
    n_rad = lax.axis_size("rad")
    slots = block_mass.shape[2]
    width = block_mass.shape[3]
    total_rows = CA * n_az
    start = sector * CA
    values = jnp.concatenate([block_mass[0, 0][:, None, :], block_flux[0, 0]], axis=1)
    dest = block_dest[0, 0]
    slot_index = jnp.arange(slots, dtype=jnp.int32)
    live = slot_index < block_count[0, 0]
    raw = local_rows(values, dest, live, start, total_rows, width)
    center, edges = window(raw)
    glob_cells = (band_index * width + jnp.arange(width, dtype=jnp.int32)).astype(jnp.float32)
    radius = width * n_rad + glob_cells + 0.5
    dtheta = 2.0 * math.pi / total_rows
    scale_az = 0.5 / (radius * dtheta)
    recip = 1.0 / radius
    xmask = ring_mask(jnp.ones((2 * width,), jnp.float32), band_index, width, n_rad)[width:]
    return stencil(center, edges, scale_az, recip, xmask)


def solution(mesh):
    return jax.shard_map(
        local,
        mesh=mesh,
        in_specs=(
            P("az", "rad", None, None),
            P("az", "rad", None, None, None),
            P("az", "rad", None),
            P("az", "rad"),
        ),
        out_specs=(
            P(None, "az", None, "rad"),
            P(None, "az", None, "rad"),
            P(None, "az", None, "rad"),
        ),
        check_vma=False,
    )
```

```python
import math

import jax
import jax.numpy as jnp
from jax import lax
from jax.experimental import pallas as pl
from jax.experimental.pallas import tpu as pltpu
from jax.sharding import PartitionSpec as P

CA = 8
H = 32
HALO = 2


density_base = 0.5


def shifted(value, da, db):
    n_az = lax.axis_size("az")
    n_rad = lax.axis_size("rad")
    pairs = []
    for a in range(n_az):
        for b in range(n_rad):
            tb = b + db
            if 0 <= tb < n_rad:
                pairs.append((a * n_rad + b, ((a + da) % n_az) * n_rad + tb))
    shape = value.shape
    if shape[-1] % 128 == 0:
        return lax.ppermute(value, ("az", "rad"), pairs)
    dense = value.reshape(value.size // 128, 128)
    return lax.ppermute(dense, ("az", "rad"), pairs).reshape(shape)


def deposit(onehot, values):
    out = jnp.einsum("ls,scn->lcn", onehot, values, precision=lax.Precision.HIGHEST)
    return jnp.transpose(out, (1, 0, 2))


def local_rows(values, dest, live, start, total_rows, width):
    local_row = jnp.mod(dest // H - start + HALO, total_rows)
    line = local_row * H + dest % H
    onehot = (
        (jnp.arange((CA + 2 * HALO) * H, dtype=jnp.int32)[:, None] == line[None, :]) & live[None, :]
    ).astype(jnp.float32)
    return deposit(onehot, values).reshape(10, CA + 2 * HALO, H, width)


def add_rows(base, head, tail):
    k = head.shape[1]
    rows = base.shape[1]
    return jnp.concatenate(
        [base[:, :k] + head, base[:, k : rows - k], base[:, rows - k :] + tail], axis=1
    )


def selector(cells, picks):
    return (jnp.arange(cells, dtype=jnp.int32)[None, :] == jnp.array(picks, jnp.int32)[:, None]).astype(
        jnp.float32
    )


def placed(values, sel):
    hi = lax.reduce_precision(values, exponent_bits=8, mantissa_bits=7)
    rest = values - hi
    mid = lax.reduce_precision(rest, exponent_bits=8, mantissa_bits=7)
    parts = jnp.concatenate([hi, mid, rest - mid], axis=0).astype(jnp.bfloat16)
    sel3 = jnp.concatenate([sel] * 3, axis=0).astype(jnp.bfloat16)
    return jnp.einsum("jm,jn->mn", parts, sel3, preferred_element_type=jnp.float32)


def window(raw):
    k = 2 * HALO
    center = add_rows(raw, shifted(raw[:, -k:], 1, 0), shifted(raw[:, :k], -1, 0))
    shape = center.shape
    cells = shape[3]
    flat = center.reshape(-1, cells)
    edge_cells = list(range(HALO)) + list(range(cells - HALO, cells))
    picked = jnp.einsum(
        "jn,mn->jm", selector(cells, edge_cells), flat, precision=lax.Precision.HIGHEST
    )
    right = shifted(picked[:HALO], 0, -1)
    left = shifted(picked[HALO:], 0, 1)
    edges = placed(jnp.concatenate([right, left], axis=0), selector(cells, edge_cells))
    return center, edges.reshape(shape)


def smooth_block(extended):
    fields = 0.25 * extended[:, :-2] + 0.5 * extended[:, 1:-1] + 0.25 * extended[:, 2:]
    fields = 0.25 * jnp.roll(fields, 1, 3) + 0.5 * fields + 0.25 * jnp.roll(fields, -1, 3)
    padded = jnp.pad(fields, ((0, 0), (0, 0), (1, 1), (0, 0)))
    return 0.25 * padded[:, :, :-2] + 0.5 * padded[:, :, 1:-1] + 0.25 * padded[:, :, 2:]


def ring_mask(extended, band_index, width, n_rad):
    lane = jnp.arange(2 * width, dtype=jnp.int32)
    columns = band_index * width + jnp.where(lane < width + width // 2, lane, lane - 2 * width)
    inside = (columns >= 0) & (columns < width * n_rad)
    return extended * inside.astype(jnp.float32)


def gradients(extended, scale_az, width):
    center = extended[:, 1:-1, :, :width]
    grad_az = (extended[:, 2:, :, :width] - extended[:, :-2, :, :width]) * scale_az
    grad_rad = (
        jnp.roll(extended[:, 1:-1], -1, 3)[..., :width] - jnp.roll(extended[:, 1:-1], 1, 3)[..., :width]
    ) * 0.5
    padded = jnp.pad(center, ((0, 0), (0, 0), (1, 1), (0, 0)))
    grad_height = (padded[:, :, 2:] - padded[:, :, :-2]) * 0.5
    return (grad_az, grad_height, grad_rad, center)


def assemble(grad_az, grad_height, grad_rad, center, recip):
    force = jnp.stack(
        [
            grad_az[3] + grad_height[6] + grad_rad[7] + 2.0 * center[7] * recip,
            grad_az[6] + grad_height[4] + grad_rad[8],
            grad_az[7] + grad_height[8] + grad_rad[5] + (center[5] - center[3]) * recip,
        ]
    )
    strain = jnp.stack(
        [
            grad_az[0] + center[2] * recip,
            grad_height[1],
            grad_rad[2],
            0.5 * (grad_height[0] + grad_az[1]),
            0.5 * (grad_rad[0] + grad_az[2] - center[0] * recip),
            0.5 * (grad_rad[1] + grad_height[2]),
        ]
    )
    return (force, strain)


def stencil_kernel(c_ref, x_ref, scale_ref, recip_ref, xmask_ref, sm_ref, force_ref, strain_ref, sc_ref, sx_ref):
    rows, height, cells = sc_ref.shape[1:]
    lane = lax.broadcasted_iota(jnp.int32, (height, cells), 1)
    sub = lax.broadcasted_iota(jnp.int32, (height, cells), 0)

    def ring(cc, xx, shift, edge):
        rc = pltpu.roll(cc, shift, 1)
        rx = pltpu.roll(xx, shift, 1)
        return jnp.where(lane == edge, rx, rc), jnp.where(lane == edge, rc, rx)

    def below(f):
        return jnp.where(sub == 0, 0.0, pltpu.roll(f, 1, 0))

    def above(f):
        return jnp.where(sub == height - 1, 0.0, pltpu.roll(f, height - 1, 0))

    def hsmooth(f):
        return 0.25 * below(f) + 0.5 * f + 0.25 * above(f)

    def smooth_channel(c, carry):
        wc = [c_ref[c, j] for j in range(rows + 2)]
        wx = [x_ref[c, j] for j in range(rows + 2)]
        for j in range(rows):
            f1c = 0.25 * wc[j] + 0.5 * wc[j + 1] + 0.25 * wc[j + 2]
            f1x = 0.25 * wx[j] + 0.5 * wx[j + 1] + 0.25 * wx[j + 2]
            pc, px = ring(f1c, f1x, 1, 0)
            nc, nx = ring(f1c, f1x, cells - 1, cells - 1)
            sc_ref[c, j] = hsmooth(0.25 * pc + 0.5 * f1c + 0.25 * nc)
            sx_ref[c, j] = hsmooth(0.25 * px + 0.5 * f1x + 0.25 * nx)
        return carry

    lax.fori_loop(0, sc_ref.shape[0], smooth_channel, 0)
    scale = scale_ref[...]
    recip = recip_ref[...]
    xmask = xmask_ref[...]

    def comb(ref, j, k):
        if k < 3:
            return ref[k + 1, j] / (ref[0, j] + density_base)
        return ref[k + 1, j]

    def out_row(r, carry):
        for c in range(sm_ref.shape[0]):
            sm_ref[c, r] = sc_ref[c, r + 1]
        center = [comb(sc_ref, r + 1, k) for k in range(9)]
        grad_az = {}
        for k in (0, 1, 2, 3, 6, 7):
            grad_az[k] = (comb(sc_ref, r + 2, k) - comb(sc_ref, r, k)) * scale
        grad_height = {k: (above(center[k]) - below(center[k])) * 0.5 for k in (0, 1, 2, 4, 6, 8)}
        grad_rad = {}
        for k in (0, 1, 2, 5, 7, 8):
            edge = comb(sx_ref, r + 1, k) * xmask
            pc, _ = ring(center[k], edge, 1, 0)
            nc, _ = ring(center[k], edge, cells - 1, cells - 1)
            grad_rad[k] = (nc - pc) * 0.5
        force_ref[0, r] = grad_az[3] + grad_height[6] + grad_rad[7] + 2.0 * center[7] * recip
        force_ref[1, r] = grad_az[6] + grad_height[4] + grad_rad[8]
        force_ref[2, r] = grad_az[7] + grad_height[8] + grad_rad[5] + (center[5] - center[3]) * recip
        strain_ref[0, r] = grad_az[0] + center[2] * recip
        strain_ref[1, r] = grad_height[1]
        strain_ref[2, r] = grad_rad[2]
        strain_ref[3, r] = 0.5 * (grad_height[0] + grad_az[1])
        strain_ref[4, r] = 0.5 * (grad_rad[0] + grad_az[2] - center[0] * recip)
        strain_ref[5, r] = 0.5 * (grad_rad[1] + grad_height[2])
        return carry

    lax.fori_loop(0, sm_ref.shape[1], out_row, 0)


def stencil(center, edges, scale_az, recip, xmask):
    channels, rows, height, cells = center.shape
    own = rows - 2 * HALO
    vmem = pl.BlockSpec(memory_space=pltpu.VMEM)
    shape = lambda n: jax.ShapeDtypeStruct((n, own, height, cells), jnp.float32)
    return pl.pallas_call(
        stencil_kernel,
        out_shape=(shape(channels), shape(3), shape(6)),
        in_specs=[vmem] * 5,
        out_specs=(vmem, vmem, vmem),
        scratch_shapes=[pltpu.VMEM((channels, rows - 2, height, cells), jnp.float32)] * 2,
    )(center, edges, scale_az.reshape(1, cells), recip.reshape(1, cells), xmask.reshape(1, cells))


def local(block_mass, block_flux, block_dest, block_count):
    sector = lax.axis_index("az")
    band_index = lax.axis_index("rad")
    n_az = lax.axis_size("az")
    n_rad = lax.axis_size("rad")
    slots = block_mass.shape[2]
    width = block_mass.shape[3]
    total_rows = CA * n_az
    start = sector * CA
    values = jnp.concatenate([block_mass[0, 0][:, None, :], block_flux[0, 0]], axis=1)
    dest = block_dest[0, 0]
    slot_index = jnp.arange(slots, dtype=jnp.int32)
    live = slot_index < block_count[0, 0]
    raw = local_rows(values, dest, live, start, total_rows, width)
    center, edges = window(raw)
    glob_cells = (band_index * width + jnp.arange(width, dtype=jnp.int32)).astype(jnp.float32)
    radius = width * n_rad + glob_cells + 0.5
    dtheta = 2.0 * math.pi / total_rows
    scale_az = 0.5 / (radius * dtheta)
    recip = 1.0 / radius
    xmask = ring_mask(jnp.ones((2 * width,), jnp.float32), band_index, width, n_rad)[width:]
    return stencil(center, edges, scale_az, recip, xmask)


def solution(mesh):
    return jax.shard_map(
        local,
        mesh=mesh,
        in_specs=(
            P("az", "rad", None, None),
            P("az", "rad", None, None, None),
            P("az", "rad", None),
            P("az", "rad"),
        ),
        out_specs=(
            P(None, "az", None, "rad"),
            P(None, "az", None, "rad"),
            P(None, "az", None, "rad"),
        ),
        check_vma=False,
    )
```

```python
import math

import jax
import jax.numpy as jnp
from jax import lax
from jax.experimental import pallas as pl
from jax.experimental.pallas import tpu as pltpu
from jax.sharding import PartitionSpec as P

CA = 8
H = 32
HALO = 2


density_base = 0.5


def shifted(value, da, db):
    n_az = lax.axis_size("az")
    n_rad = lax.axis_size("rad")
    pairs = []
    for a in range(n_az):
        for b in range(n_rad):
            tb = b + db
            if 0 <= tb < n_rad:
                pairs.append((a * n_rad + b, ((a + da) % n_az) * n_rad + tb))
    shape = value.shape
    if shape[-1] % 128 == 0:
        return lax.ppermute(value, ("az", "rad"), pairs)
    dense = value.reshape(value.size // 128, 128)
    return lax.ppermute(dense, ("az", "rad"), pairs).reshape(shape)


def deposit(onehot, values):
    hi = lax.reduce_precision(values, exponent_bits=8, mantissa_bits=7)
    rest = values - hi
    mid = lax.reduce_precision(rest, exponent_bits=8, mantissa_bits=7)
    parts = jnp.concatenate([hi, mid, rest - mid], axis=0).astype(jnp.bfloat16)
    lines = jnp.concatenate([onehot] * 3, axis=1).astype(jnp.bfloat16)
    out = jnp.einsum("ls,scn->lcn", lines, parts, preferred_element_type=jnp.float32)
    return jnp.transpose(out, (1, 0, 2))


def local_rows(values, dest, live, start, total_rows, width):
    local_row = jnp.mod(dest // H - start + HALO, total_rows)
    line = local_row * H + dest % H
    onehot = (
        (jnp.arange((CA + 2 * HALO) * H, dtype=jnp.int32)[:, None] == line[None, :]) & live[None, :]
    ).astype(jnp.float32)
    return deposit(onehot, values).reshape(10, CA + 2 * HALO, H, width)


def add_rows(base, head, tail):
    k = head.shape[1]
    rows = base.shape[1]
    return jnp.concatenate(
        [base[:, :k] + head, base[:, k : rows - k], base[:, rows - k :] + tail], axis=1
    )


def selector(cells, picks):
    return (jnp.arange(cells, dtype=jnp.int32)[None, :] == jnp.array(picks, jnp.int32)[:, None]).astype(
        jnp.float32
    )


def placed(values, sel):
    hi = lax.reduce_precision(values, exponent_bits=8, mantissa_bits=7)
    rest = values - hi
    mid = lax.reduce_precision(rest, exponent_bits=8, mantissa_bits=7)
    parts = jnp.concatenate([hi, mid, rest - mid], axis=0).astype(jnp.bfloat16)
    sel3 = jnp.concatenate([sel] * 3, axis=0).astype(jnp.bfloat16)
    return jnp.einsum("jm,jn->mn", parts, sel3, preferred_element_type=jnp.float32)


def window(raw):
    k = 2 * HALO
    center = add_rows(raw, shifted(raw[:, -k:], 1, 0), shifted(raw[:, :k], -1, 0))
    shape = center.shape
    cells = shape[3]
    flat = center.reshape(-1, cells)
    edge_cells = list(range(HALO)) + list(range(cells - HALO, cells))
    picked = jnp.einsum(
        "jn,mn->jm", selector(cells, edge_cells), flat, precision=lax.Precision.HIGHEST
    )
    right = shifted(picked[:HALO], 0, -1)
    left = shifted(picked[HALO:], 0, 1)
    edges = placed(jnp.concatenate([right, left], axis=0), selector(cells, edge_cells))
    return center, edges.reshape(shape)


def smooth_block(extended):
    fields = 0.25 * extended[:, :-2] + 0.5 * extended[:, 1:-1] + 0.25 * extended[:, 2:]
    fields = 0.25 * jnp.roll(fields, 1, 3) + 0.5 * fields + 0.25 * jnp.roll(fields, -1, 3)
    padded = jnp.pad(fields, ((0, 0), (0, 0), (1, 1), (0, 0)))
    return 0.25 * padded[:, :, :-2] + 0.5 * padded[:, :, 1:-1] + 0.25 * padded[:, :, 2:]


def ring_mask(extended, band_index, width, n_rad):
    lane = jnp.arange(2 * width, dtype=jnp.int32)
    columns = band_index * width + jnp.where(lane < width + width // 2, lane, lane - 2 * width)
    inside = (columns >= 0) & (columns < width * n_rad)
    return extended * inside.astype(jnp.float32)


def gradients(extended, scale_az, width):
    center = extended[:, 1:-1, :, :width]
    grad_az = (extended[:, 2:, :, :width] - extended[:, :-2, :, :width]) * scale_az
    grad_rad = (
        jnp.roll(extended[:, 1:-1], -1, 3)[..., :width] - jnp.roll(extended[:, 1:-1], 1, 3)[..., :width]
    ) * 0.5
    padded = jnp.pad(center, ((0, 0), (0, 0), (1, 1), (0, 0)))
    grad_height = (padded[:, :, 2:] - padded[:, :, :-2]) * 0.5
    return (grad_az, grad_height, grad_rad, center)


def assemble(grad_az, grad_height, grad_rad, center, recip):
    force = jnp.stack(
        [
            grad_az[3] + grad_height[6] + grad_rad[7] + 2.0 * center[7] * recip,
            grad_az[6] + grad_height[4] + grad_rad[8],
            grad_az[7] + grad_height[8] + grad_rad[5] + (center[5] - center[3]) * recip,
        ]
    )
    strain = jnp.stack(
        [
            grad_az[0] + center[2] * recip,
            grad_height[1],
            grad_rad[2],
            0.5 * (grad_height[0] + grad_az[1]),
            0.5 * (grad_rad[0] + grad_az[2] - center[0] * recip),
            0.5 * (grad_rad[1] + grad_height[2]),
        ]
    )
    return (force, strain)


def stencil_kernel(c_ref, x_ref, scale_ref, recip_ref, xmask_ref, sm_ref, force_ref, strain_ref, sc_ref, sx_ref):
    rows, height, cells = sc_ref.shape[1:]
    lane = lax.broadcasted_iota(jnp.int32, (height, cells), 1)
    sub = lax.broadcasted_iota(jnp.int32, (height, cells), 0)

    def ring(cc, xx, shift, edge):
        rc = pltpu.roll(cc, shift, 1)
        rx = pltpu.roll(xx, shift, 1)
        return jnp.where(lane == edge, rx, rc), jnp.where(lane == edge, rc, rx)

    def below(f):
        return jnp.where(sub == 0, 0.0, pltpu.roll(f, 1, 0))

    def above(f):
        return jnp.where(sub == height - 1, 0.0, pltpu.roll(f, height - 1, 0))

    def hsmooth(f):
        return 0.25 * below(f) + 0.5 * f + 0.25 * above(f)

    def smooth_channel(c, carry):
        wc = [c_ref[c, j] for j in range(rows + 2)]
        wx = [x_ref[c, j] for j in range(rows + 2)]
        for j in range(rows):
            f1c = 0.25 * wc[j] + 0.5 * wc[j + 1] + 0.25 * wc[j + 2]
            f1x = 0.25 * wx[j] + 0.5 * wx[j + 1] + 0.25 * wx[j + 2]
            pc, px = ring(f1c, f1x, 1, 0)
            nc, nx = ring(f1c, f1x, cells - 1, cells - 1)
            sc_ref[c, j] = hsmooth(0.25 * pc + 0.5 * f1c + 0.25 * nc)
            sx_ref[c, j] = hsmooth(0.25 * px + 0.5 * f1x + 0.25 * nx)
        return carry

    lax.fori_loop(0, sc_ref.shape[0], smooth_channel, 0)
    scale = scale_ref[...]
    recip = recip_ref[...]
    xmask = xmask_ref[...]

    def comb(ref, j, k):
        if k < 3:
            return ref[k + 1, j] / (ref[0, j] + density_base)
        return ref[k + 1, j]

    def out_row(r, carry):
        for c in range(sm_ref.shape[0]):
            sm_ref[c, r] = sc_ref[c, r + 1]
        center = [comb(sc_ref, r + 1, k) for k in range(9)]
        grad_az = {}
        for k in (0, 1, 2, 3, 6, 7):
            grad_az[k] = (comb(sc_ref, r + 2, k) - comb(sc_ref, r, k)) * scale
        grad_height = {k: (above(center[k]) - below(center[k])) * 0.5 for k in (0, 1, 2, 4, 6, 8)}
        grad_rad = {}
        for k in (0, 1, 2, 5, 7, 8):
            edge = comb(sx_ref, r + 1, k) * xmask
            pc, _ = ring(center[k], edge, 1, 0)
            nc, _ = ring(center[k], edge, cells - 1, cells - 1)
            grad_rad[k] = (nc - pc) * 0.5
        force_ref[0, r] = grad_az[3] + grad_height[6] + grad_rad[7] + 2.0 * center[7] * recip
        force_ref[1, r] = grad_az[6] + grad_height[4] + grad_rad[8]
        force_ref[2, r] = grad_az[7] + grad_height[8] + grad_rad[5] + (center[5] - center[3]) * recip
        strain_ref[0, r] = grad_az[0] + center[2] * recip
        strain_ref[1, r] = grad_height[1]
        strain_ref[2, r] = grad_rad[2]
        strain_ref[3, r] = 0.5 * (grad_height[0] + grad_az[1])
        strain_ref[4, r] = 0.5 * (grad_rad[0] + grad_az[2] - center[0] * recip)
        strain_ref[5, r] = 0.5 * (grad_rad[1] + grad_height[2])
        return carry

    lax.fori_loop(0, sm_ref.shape[1], out_row, 0)


def stencil(center, edges, scale_az, recip, xmask):
    channels, rows, height, cells = center.shape
    own = rows - 2 * HALO
    vmem = pl.BlockSpec(memory_space=pltpu.VMEM)
    shape = lambda n: jax.ShapeDtypeStruct((n, own, height, cells), jnp.float32)
    return pl.pallas_call(
        stencil_kernel,
        out_shape=(shape(channels), shape(3), shape(6)),
        in_specs=[vmem] * 5,
        out_specs=(vmem, vmem, vmem),
        scratch_shapes=[pltpu.VMEM((channels, rows - 2, height, cells), jnp.float32)] * 2,
    )(center, edges, scale_az.reshape(1, cells), recip.reshape(1, cells), xmask.reshape(1, cells))


def local(block_mass, block_flux, block_dest, block_count):
    sector = lax.axis_index("az")
    band_index = lax.axis_index("rad")
    n_az = lax.axis_size("az")
    n_rad = lax.axis_size("rad")
    slots = block_mass.shape[2]
    width = block_mass.shape[3]
    total_rows = CA * n_az
    start = sector * CA
    values = jnp.concatenate([block_mass[0, 0][:, None, :], block_flux[0, 0]], axis=1)
    dest = block_dest[0, 0]
    slot_index = jnp.arange(slots, dtype=jnp.int32)
    live = slot_index < block_count[0, 0]
    raw = local_rows(values, dest, live, start, total_rows, width)
    center, edges = window(raw)
    glob_cells = (band_index * width + jnp.arange(width, dtype=jnp.int32)).astype(jnp.float32)
    radius = width * n_rad + glob_cells + 0.5
    dtheta = 2.0 * math.pi / total_rows
    scale_az = 0.5 / (radius * dtheta)
    recip = 1.0 / radius
    xmask = ring_mask(jnp.ones((2 * width,), jnp.float32), band_index, width, n_rad)[width:]
    return stencil(center, edges, scale_az, recip, xmask)


def solution(mesh):
    return jax.shard_map(
        local,
        mesh=mesh,
        in_specs=(
            P("az", "rad", None, None),
            P("az", "rad", None, None, None),
            P("az", "rad", None),
            P("az", "rad"),
        ),
        out_specs=(
            P(None, "az", None, "rad"),
            P(None, "az", None, "rad"),
            P(None, "az", None, "rad"),
        ),
        check_vma=False,
    )
```

```python
import math

import jax
import jax.numpy as jnp
from jax import lax
from jax.experimental import pallas as pl
from jax.experimental.pallas import tpu as pltpu
from jax.sharding import PartitionSpec as P

CA = 8
H = 32
HALO = 2


density_base = 0.5


def shifted(value, da, db):
    n_az = lax.axis_size("az")
    n_rad = lax.axis_size("rad")
    pairs = []
    for a in range(n_az):
        for b in range(n_rad):
            tb = b + db
            if 0 <= tb < n_rad:
                pairs.append((a * n_rad + b, ((a + da) % n_az) * n_rad + tb))
    shape = value.shape
    if shape[-1] % 128 == 0:
        return lax.ppermute(value, ("az", "rad"), pairs)
    dense = value.reshape(value.size // 128, 128)
    return lax.ppermute(dense, ("az", "rad"), pairs).reshape(shape)


def deposit(onehot, values):
    out = jnp.einsum("ls,scn->lcn", onehot, values, precision=lax.Precision.HIGHEST)
    return jnp.transpose(out, (1, 0, 2))


def local_rows(values, dest, live, start, total_rows, width, lines):
    local_row = jnp.mod(dest // H - start + HALO, total_rows)
    line = local_row * H + dest % H
    onehot = ((lines[:, None] == line[None, :]) & live[None, :]).astype(jnp.float32)
    return deposit(onehot, values).reshape(10, -1, H, width)


def add_rows(base, head, tail):
    k = head.shape[1]
    rows = base.shape[1]
    return jnp.concatenate(
        [base[:, :k] + head, base[:, k : rows - k], base[:, rows - k :] + tail], axis=1
    )


def selector(cells, picks):
    return (jnp.arange(cells, dtype=jnp.int32)[None, :] == jnp.array(picks, jnp.int32)[:, None]).astype(
        jnp.float32
    )


def placed(values, sel):
    hi = lax.reduce_precision(values, exponent_bits=8, mantissa_bits=7)
    rest = values - hi
    mid = lax.reduce_precision(rest, exponent_bits=8, mantissa_bits=7)
    parts = jnp.concatenate([hi, mid, rest - mid], axis=0).astype(jnp.bfloat16)
    sel3 = jnp.concatenate([sel] * 3, axis=0).astype(jnp.bfloat16)
    return jnp.einsum("jm,jn->mn", parts, sel3, preferred_element_type=jnp.float32)


def window(raw, top, bottom):
    center = add_rows(raw, shifted(bottom, 1, 0), shifted(top, -1, 0))
    shape = center.shape
    cells = shape[3]
    flat = center.reshape(-1, cells)
    edge_cells = list(range(HALO)) + list(range(cells - HALO, cells))
    picked = jnp.einsum(
        "jn,mn->jm", selector(cells, edge_cells), flat, precision=lax.Precision.HIGHEST
    )
    right = shifted(picked[:HALO], 0, -1)
    left = shifted(picked[HALO:], 0, 1)
    edges = placed(jnp.concatenate([right, left], axis=0), selector(cells, edge_cells))
    return center, edges.reshape(shape)


def smooth_block(extended):
    fields = 0.25 * extended[:, :-2] + 0.5 * extended[:, 1:-1] + 0.25 * extended[:, 2:]
    fields = 0.25 * jnp.roll(fields, 1, 3) + 0.5 * fields + 0.25 * jnp.roll(fields, -1, 3)
    padded = jnp.pad(fields, ((0, 0), (0, 0), (1, 1), (0, 0)))
    return 0.25 * padded[:, :, :-2] + 0.5 * padded[:, :, 1:-1] + 0.25 * padded[:, :, 2:]


def ring_mask(extended, band_index, width, n_rad):
    lane = jnp.arange(2 * width, dtype=jnp.int32)
    columns = band_index * width + jnp.where(lane < width + width // 2, lane, lane - 2 * width)
    inside = (columns >= 0) & (columns < width * n_rad)
    return extended * inside.astype(jnp.float32)


def gradients(extended, scale_az, width):
    center = extended[:, 1:-1, :, :width]
    grad_az = (extended[:, 2:, :, :width] - extended[:, :-2, :, :width]) * scale_az
    grad_rad = (
        jnp.roll(extended[:, 1:-1], -1, 3)[..., :width] - jnp.roll(extended[:, 1:-1], 1, 3)[..., :width]
    ) * 0.5
    padded = jnp.pad(center, ((0, 0), (0, 0), (1, 1), (0, 0)))
    grad_height = (padded[:, :, 2:] - padded[:, :, :-2]) * 0.5
    return (grad_az, grad_height, grad_rad, center)


def assemble(grad_az, grad_height, grad_rad, center, recip):
    force = jnp.stack(
        [
            grad_az[3] + grad_height[6] + grad_rad[7] + 2.0 * center[7] * recip,
            grad_az[6] + grad_height[4] + grad_rad[8],
            grad_az[7] + grad_height[8] + grad_rad[5] + (center[5] - center[3]) * recip,
        ]
    )
    strain = jnp.stack(
        [
            grad_az[0] + center[2] * recip,
            grad_height[1],
            grad_rad[2],
            0.5 * (grad_height[0] + grad_az[1]),
            0.5 * (grad_rad[0] + grad_az[2] - center[0] * recip),
            0.5 * (grad_rad[1] + grad_height[2]),
        ]
    )
    return (force, strain)


def stencil_kernel(c_ref, x_ref, scale_ref, recip_ref, xmask_ref, sm_ref, force_ref, strain_ref, sc_ref, sx_ref):
    rows, height, cells = sc_ref.shape[1:]
    lane = lax.broadcasted_iota(jnp.int32, (height, cells), 1)
    sub = lax.broadcasted_iota(jnp.int32, (height, cells), 0)

    def ring(cc, xx, shift, edge):
        rc = pltpu.roll(cc, shift, 1)
        rx = pltpu.roll(xx, shift, 1)
        return jnp.where(lane == edge, rx, rc), jnp.where(lane == edge, rc, rx)

    def below(f):
        return jnp.where(sub == 0, 0.0, pltpu.roll(f, 1, 0))

    def above(f):
        return jnp.where(sub == height - 1, 0.0, pltpu.roll(f, height - 1, 0))

    def hsmooth(f):
        return 0.25 * below(f) + 0.5 * f + 0.25 * above(f)

    def smooth_channel(c, carry):
        wc = [c_ref[c, j] for j in range(rows + 2)]
        wx = [x_ref[c, j] for j in range(rows + 2)]
        for j in range(rows):
            f1c = 0.25 * wc[j] + 0.5 * wc[j + 1] + 0.25 * wc[j + 2]
            f1x = 0.25 * wx[j] + 0.5 * wx[j + 1] + 0.25 * wx[j + 2]
            pc, px = ring(f1c, f1x, 1, 0)
            nc, nx = ring(f1c, f1x, cells - 1, cells - 1)
            sc_ref[c, j] = hsmooth(0.25 * pc + 0.5 * f1c + 0.25 * nc)
            sx_ref[c, j] = hsmooth(0.25 * px + 0.5 * f1x + 0.25 * nx)
        return carry

    lax.fori_loop(0, sc_ref.shape[0], smooth_channel, 0)
    scale = scale_ref[...]
    recip = recip_ref[...]
    xmask = xmask_ref[...]

    def comb(ref, j, k):
        if k < 3:
            return ref[k + 1, j] / (ref[0, j] + density_base)
        return ref[k + 1, j]

    def out_row(r, carry):
        for c in range(sm_ref.shape[0]):
            sm_ref[c, r] = sc_ref[c, r + 1]
        center = [comb(sc_ref, r + 1, k) for k in range(9)]
        grad_az = {}
        for k in (0, 1, 2, 3, 6, 7):
            grad_az[k] = (comb(sc_ref, r + 2, k) - comb(sc_ref, r, k)) * scale
        grad_height = {k: (above(center[k]) - below(center[k])) * 0.5 for k in (0, 1, 2, 4, 6, 8)}
        grad_rad = {}
        for k in (0, 1, 2, 5, 7, 8):
            edge = comb(sx_ref, r + 1, k) * xmask
            pc, _ = ring(center[k], edge, 1, 0)
            nc, _ = ring(center[k], edge, cells - 1, cells - 1)
            grad_rad[k] = (nc - pc) * 0.5
        force_ref[0, r] = grad_az[3] + grad_height[6] + grad_rad[7] + 2.0 * center[7] * recip
        force_ref[1, r] = grad_az[6] + grad_height[4] + grad_rad[8]
        force_ref[2, r] = grad_az[7] + grad_height[8] + grad_rad[5] + (center[5] - center[3]) * recip
        strain_ref[0, r] = grad_az[0] + center[2] * recip
        strain_ref[1, r] = grad_height[1]
        strain_ref[2, r] = grad_rad[2]
        strain_ref[3, r] = 0.5 * (grad_height[0] + grad_az[1])
        strain_ref[4, r] = 0.5 * (grad_rad[0] + grad_az[2] - center[0] * recip)
        strain_ref[5, r] = 0.5 * (grad_rad[1] + grad_height[2])
        return carry

    lax.fori_loop(0, sm_ref.shape[1], out_row, 0)


def stencil(center, edges, scale_az, recip, xmask):
    channels, rows, height, cells = center.shape
    own = rows - 2 * HALO
    vmem = pl.BlockSpec(memory_space=pltpu.VMEM)
    shape = lambda n: jax.ShapeDtypeStruct((n, own, height, cells), jnp.float32)
    return pl.pallas_call(
        stencil_kernel,
        out_shape=(shape(channels), shape(3), shape(6)),
        in_specs=[vmem] * 5,
        out_specs=(vmem, vmem, vmem),
        scratch_shapes=[pltpu.VMEM((channels, rows - 2, height, cells), jnp.float32)] * 2,
    )(center, edges, scale_az.reshape(1, cells), recip.reshape(1, cells), xmask.reshape(1, cells))


def local(block_mass, block_flux, block_dest, block_count):
    sector = lax.axis_index("az")
    band_index = lax.axis_index("rad")
    n_az = lax.axis_size("az")
    n_rad = lax.axis_size("rad")
    slots = block_mass.shape[2]
    width = block_mass.shape[3]
    total_rows = CA * n_az
    start = sector * CA
    values = jnp.concatenate([block_mass[0, 0][:, None, :], block_flux[0, 0]], axis=1)
    dest = block_dest[0, 0]
    slot_index = jnp.arange(slots, dtype=jnp.int32)
    live = slot_index < block_count[0, 0]
    lines = jnp.arange((CA + 2 * HALO) * H, dtype=jnp.int32)
    k = 2 * HALO * H
    deposited = lambda part: local_rows(values, dest, live, start, total_rows, width, part)
    center, edges = window(deposited(lines), deposited(lines[:k]), deposited(lines[-k:]))
    glob_cells = (band_index * width + jnp.arange(width, dtype=jnp.int32)).astype(jnp.float32)
    radius = width * n_rad + glob_cells + 0.5
    dtheta = 2.0 * math.pi / total_rows
    scale_az = 0.5 / (radius * dtheta)
    recip = 1.0 / radius
    xmask = ring_mask(jnp.ones((2 * width,), jnp.float32), band_index, width, n_rad)[width:]
    return stencil(center, edges, scale_az, recip, xmask)


def solution(mesh):
    return jax.shard_map(
        local,
        mesh=mesh,
        in_specs=(
            P("az", "rad", None, None),
            P("az", "rad", None, None, None),
            P("az", "rad", None),
            P("az", "rad"),
        ),
        out_specs=(
            P(None, "az", None, "rad"),
            P(None, "az", None, "rad"),
            P(None, "az", None, "rad"),
        ),
        check_vma=False,
    )
```

```python
import math

import jax
import jax.numpy as jnp
from jax import lax
from jax.experimental import pallas as pl
from jax.experimental.pallas import tpu as pltpu
from jax.sharding import PartitionSpec as P

CA = 8
H = 32
HALO = 2


density_base = 0.5


def shifted(value, da, db):
    n_az = lax.axis_size("az")
    n_rad = lax.axis_size("rad")
    pairs = []
    for a in range(n_az):
        for b in range(n_rad):
            tb = b + db
            if 0 <= tb < n_rad:
                pairs.append((a * n_rad + b, ((a + da) % n_az) * n_rad + tb))
    shape = value.shape
    if shape[-1] % 128 == 0:
        return lax.ppermute(value, ("az", "rad"), pairs)
    dense = value.reshape(value.size // 128, 128)
    return lax.ppermute(dense, ("az", "rad"), pairs).reshape(shape)


def deposit(onehot, values):
    out = jnp.einsum("ls,scn->lcn", onehot, values, precision=lax.Precision.HIGHEST)
    return jnp.transpose(out, (1, 0, 2))


def local_rows(values, dest, live, start, total_rows, width):
    local_row = jnp.mod(dest // H - start + HALO, total_rows)
    line = local_row * H + dest % H
    onehot = (
        (jnp.arange((CA + 2 * HALO) * H, dtype=jnp.int32)[:, None] == line[None, :]) & live[None, :]
    ).astype(jnp.float32)
    return deposit(onehot, values).reshape(10, CA + 2 * HALO, H, width)


def add_rows(base, head, tail):
    k = head.shape[1]
    rows = base.shape[1]
    return jnp.concatenate(
        [base[:, :k] + head, base[:, k : rows - k], base[:, rows - k :] + tail], axis=1
    )


def selector(cells, picks):
    return (jnp.arange(cells, dtype=jnp.int32)[None, :] == jnp.array(picks, jnp.int32)[:, None]).astype(
        jnp.float32
    )


def placed(values, sel):
    hi = lax.reduce_precision(values, exponent_bits=8, mantissa_bits=7)
    rest = values - hi
    mid = lax.reduce_precision(rest, exponent_bits=8, mantissa_bits=7)
    parts = jnp.concatenate([hi, mid, rest - mid], axis=0).astype(jnp.bfloat16)
    sel3 = jnp.concatenate([sel] * 3, axis=0).astype(jnp.bfloat16)
    return jnp.einsum("jm,jn->mn", parts, sel3, preferred_element_type=jnp.float32)


def window(raw):
    k = 2 * HALO
    center = add_rows(raw, shifted(raw[:, -k:], 1, 0), shifted(raw[:, :k], -1, 0))
    shape = center.shape
    cells = shape[3]
    flat = center.reshape(-1, cells)
    edge_cells = list(range(HALO)) + list(range(cells - HALO, cells))
    picked = jnp.einsum(
        "jn,mn->jm", selector(cells, edge_cells), flat, precision=lax.Precision.HIGHEST
    )
    right = shifted(picked[:HALO], 0, -1)
    left = shifted(picked[HALO:], 0, 1)
    edges = placed(jnp.concatenate([right, left], axis=0), selector(cells, edge_cells))
    return center, edges.reshape(shape)


def smooth_block(extended):
    fields = 0.25 * extended[:, :-2] + 0.5 * extended[:, 1:-1] + 0.25 * extended[:, 2:]
    fields = 0.25 * jnp.roll(fields, 1, 3) + 0.5 * fields + 0.25 * jnp.roll(fields, -1, 3)
    padded = jnp.pad(fields, ((0, 0), (0, 0), (1, 1), (0, 0)))
    return 0.25 * padded[:, :, :-2] + 0.5 * padded[:, :, 1:-1] + 0.25 * padded[:, :, 2:]


def ring_mask(extended, band_index, width, n_rad):
    lane = jnp.arange(2 * width, dtype=jnp.int32)
    columns = band_index * width + jnp.where(lane < width + width // 2, lane, lane - 2 * width)
    inside = (columns >= 0) & (columns < width * n_rad)
    return extended * inside.astype(jnp.float32)


def gradients(extended, scale_az, width):
    center = extended[:, 1:-1, :, :width]
    grad_az = (extended[:, 2:, :, :width] - extended[:, :-2, :, :width]) * scale_az
    grad_rad = (
        jnp.roll(extended[:, 1:-1], -1, 3)[..., :width] - jnp.roll(extended[:, 1:-1], 1, 3)[..., :width]
    ) * 0.5
    padded = jnp.pad(center, ((0, 0), (0, 0), (1, 1), (0, 0)))
    grad_height = (padded[:, :, 2:] - padded[:, :, :-2]) * 0.5
    return (grad_az, grad_height, grad_rad, center)


def assemble(grad_az, grad_height, grad_rad, center, recip):
    force = jnp.stack(
        [
            grad_az[3] + grad_height[6] + grad_rad[7] + 2.0 * center[7] * recip,
            grad_az[6] + grad_height[4] + grad_rad[8],
            grad_az[7] + grad_height[8] + grad_rad[5] + (center[5] - center[3]) * recip,
        ]
    )
    strain = jnp.stack(
        [
            grad_az[0] + center[2] * recip,
            grad_height[1],
            grad_rad[2],
            0.5 * (grad_height[0] + grad_az[1]),
            0.5 * (grad_rad[0] + grad_az[2] - center[0] * recip),
            0.5 * (grad_rad[1] + grad_height[2]),
        ]
    )
    return (force, strain)


def stencil_kernel(c_ref, x_ref, scale_ref, recip_ref, xmask_ref, sm_ref, force_ref, strain_ref, sc_ref, sx_ref):
    rows, height, cells = sc_ref.shape[1:]
    lane = lax.broadcasted_iota(jnp.int32, (height, cells), 1)
    sub = lax.broadcasted_iota(jnp.int32, (height, cells), 0)

    def ring(cc, xx, shift, edge):
        rc = pltpu.roll(cc, shift, 1)
        rx = pltpu.roll(xx, shift, 1)
        return jnp.where(lane == edge, rx, rc), jnp.where(lane == edge, rc, rx)

    def below(f):
        return jnp.where(sub == 0, 0.0, pltpu.roll(f, 1, 0))

    def above(f):
        return jnp.where(sub == height - 1, 0.0, pltpu.roll(f, height - 1, 0))

    def hsmooth(f):
        return 0.25 * below(f) + 0.5 * f + 0.25 * above(f)

    def smooth_channel(c, carry):
        wc = [c_ref[c, j] for j in range(rows + 2)]
        wx = [x_ref[c, j] for j in range(rows + 2)]
        for j in range(rows):
            f1c = 0.25 * wc[j] + 0.5 * wc[j + 1] + 0.25 * wc[j + 2]
            f1x = 0.25 * wx[j] + 0.5 * wx[j + 1] + 0.25 * wx[j + 2]
            pc, px = ring(f1c, f1x, 1, 0)
            nc, nx = ring(f1c, f1x, cells - 1, cells - 1)
            smooth_c = hsmooth(0.25 * pc + 0.5 * f1c + 0.25 * nc)
            sc_ref[c, j] = smooth_c
            if 0 < j < rows - 1:
                sm_ref[c, j - 1] = smooth_c
            sx_ref[c, j] = hsmooth(0.25 * px + 0.5 * f1x + 0.25 * nx)
        return carry

    lax.fori_loop(0, sc_ref.shape[0], smooth_channel, 0)
    scale = scale_ref[...]
    recip = recip_ref[...]
    xmask = xmask_ref[...]

    def comb(ref, j, k):
        if k < 3:
            return ref[k + 1, j] / (ref[0, j] + density_base)
        return ref[k + 1, j]

    def out_row(r, carry):
        center = [comb(sc_ref, r + 1, k) for k in range(9)]
        grad_az = {}
        for k in (0, 1, 2, 3, 6, 7):
            grad_az[k] = (comb(sc_ref, r + 2, k) - comb(sc_ref, r, k)) * scale
        grad_height = {k: (above(center[k]) - below(center[k])) * 0.5 for k in (0, 1, 2, 4, 6, 8)}
        grad_rad = {}
        for k in (0, 1, 2, 5, 7, 8):
            edge = comb(sx_ref, r + 1, k) * xmask
            pc, _ = ring(center[k], edge, 1, 0)
            nc, _ = ring(center[k], edge, cells - 1, cells - 1)
            grad_rad[k] = (nc - pc) * 0.5
        force_ref[0, r] = grad_az[3] + grad_height[6] + grad_rad[7] + 2.0 * center[7] * recip
        force_ref[1, r] = grad_az[6] + grad_height[4] + grad_rad[8]
        force_ref[2, r] = grad_az[7] + grad_height[8] + grad_rad[5] + (center[5] - center[3]) * recip
        strain_ref[0, r] = grad_az[0] + center[2] * recip
        strain_ref[1, r] = grad_height[1]
        strain_ref[2, r] = grad_rad[2]
        strain_ref[3, r] = 0.5 * (grad_height[0] + grad_az[1])
        strain_ref[4, r] = 0.5 * (grad_rad[0] + grad_az[2] - center[0] * recip)
        strain_ref[5, r] = 0.5 * (grad_rad[1] + grad_height[2])
        return carry

    lax.fori_loop(0, sm_ref.shape[1], out_row, 0)


def stencil(center, edges, scale_az, recip, xmask):
    channels, rows, height, cells = center.shape
    own = rows - 2 * HALO
    vmem = pl.BlockSpec(memory_space=pltpu.VMEM)
    shape = lambda n: jax.ShapeDtypeStruct((n, own, height, cells), jnp.float32)
    return pl.pallas_call(
        stencil_kernel,
        out_shape=(shape(channels), shape(3), shape(6)),
        in_specs=[vmem] * 5,
        out_specs=(vmem, vmem, vmem),
        scratch_shapes=[pltpu.VMEM((channels, rows - 2, height, cells), jnp.float32)] * 2,
    )(center, edges, scale_az.reshape(1, cells), recip.reshape(1, cells), xmask.reshape(1, cells))


def local(block_mass, block_flux, block_dest, block_count):
    sector = lax.axis_index("az")
    band_index = lax.axis_index("rad")
    n_az = lax.axis_size("az")
    n_rad = lax.axis_size("rad")
    slots = block_mass.shape[2]
    width = block_mass.shape[3]
    total_rows = CA * n_az
    start = sector * CA
    values = jnp.concatenate([block_mass[0, 0][:, None, :], block_flux[0, 0]], axis=1)
    dest = block_dest[0, 0]
    slot_index = jnp.arange(slots, dtype=jnp.int32)
    live = slot_index < block_count[0, 0]
    raw = local_rows(values, dest, live, start, total_rows, width)
    center, edges = window(raw)
    glob_cells = (band_index * width + jnp.arange(width, dtype=jnp.int32)).astype(jnp.float32)
    radius = width * n_rad + glob_cells + 0.5
    dtheta = 2.0 * math.pi / total_rows
    scale_az = 0.5 / (radius * dtheta)
    recip = 1.0 / radius
    xmask = ring_mask(jnp.ones((2 * width,), jnp.float32), band_index, width, n_rad)[width:]
    return stencil(center, edges, scale_az, recip, xmask)


def solution(mesh):
    return jax.shard_map(
        local,
        mesh=mesh,
        in_specs=(
            P("az", "rad", None, None),
            P("az", "rad", None, None, None),
            P("az", "rad", None),
            P("az", "rad"),
        ),
        out_specs=(
            P(None, "az", None, "rad"),
            P(None, "az", None, "rad"),
            P(None, "az", None, "rad"),
        ),
        check_vma=False,
    )
```
